32 devices in a mesh: hyper: 2 (over x), row: 16 (over z, y, core).
Axes of the slice: x: 2, y: 2, z: 4, core: 2. Of those that a mesh axis runs over, the one named last changes fastest.
Arguments:
- carried_block: float32 [8192, 4096], P(('hyper', 'row')), parts along dimension 0, as said below
- coupling_values: float32 [8192, 256], P(('hyper', 'row')), parts along dimension 0, may hold values from -0.15 to 0.15
- block_cols: int32 [128, 8], P('row'), may hold values from 0 to 127, as said below
- next_block: float32 [8192, 4096], P(('hyper', 'row')), parts along dimension 0, as said below
- fixed_rows: float32 [32, 4096], P('hyper', 'row'), parts along dimension 0, may hold values from -0.1875 to 0.1875
- fixed_next: float32 [32, 4096], P('hyper', 'row'), parts along dimension 0, may hold values from -6 to 6
- tip_block: float32 [32, 16], P('hyper'), parts along dimension 0, as said below
Outputs:
- factor_state: float32 [8192, 4096], P(('hyper', 'row')), parts along dimension 0
- coupling_factor: float32 [8192, 4096], P(('hyper', 'row')), parts along dimension 0
- carried_next: float32 [8192, 4096], P(('hyper', 'row')), parts along dimension 0
- fixed_factor: float32 [32, 4096], P('hyper', 'row'), parts along dimension 0
- fixed_carried: float32 [32, 4096], P('hyper', 'row'), parts along dimension 0
- tip_next: float32 [32, 16], P('hyper'), parts along dimension 0
The draws below stay inside these ranges and needn't reach their ends.
There are 2 independent parts, one for each index of `hyper`. The reference program is written for one: setup_inputs(seed, part) draws one part's arguments, and reference() takes and returns one part's arrays. A program takes and returns all parts, laid end to end along the dimension named above; an argument that names none is the same for every part. Nothing has to cross between parts.
Inputs may be any that keep to these rules, and one draw needn't show every extreme that they name: `block_cols`: row r lists 8 distinct block columns; the first is r itself, the others lie within 32 blocks of r, cyclically. `carried_block`: symmetric positive definite. `next_block`: symmetric positive definite. `tip_block`: Symmetric.
All inputs are finite; a program needn't handle non-finite values.
Results may differ from the reference program's by a relative error of at most 0.0001.
Values sent between devices are 32-bit elements; how exact they have to be, the bound alone decides.
No kernel may reach another device: no remote copies, remote signals or barrier semaphores. Data moves between devices by JAX's collectives and lax.ppermute only.
A program may use at most 128 MiB of HBM per device.

```python
import math
import jax
import jax.numpy as jnp
from jax import lax

B = 4096
NF = 16
TILE = 32
NNZB = 8
PANELS = 4
NB = 128
N_ROW = 16


def symmetric_block(key, size, low, high):
    first, second = jax.random.split(key)
    spread = 0.7 * math.sqrt(3.0) / math.sqrt(size)
    noise = jax.random.uniform(first, (size, size), jnp.float32, -1.0, 1.0) * spread
    mirrored = (noise + noise.T) * 0.70710678
    diagonal = jax.random.uniform(second, (size,), jnp.float32, low, high)
    on_diagonal = jnp.eye(size, dtype=bool)
    return jnp.where(on_diagonal, diagonal[:, None], mirrored)


def stencil_block(key, size, stride, low, high):
    first, second, third = jax.random.split(key, 3)
    dense = symmetric_block(first, size, low, high)
    near = jax.random.uniform(second, (size, size), jnp.float32, 0.6, 0.9)
    near = (near + near.T) * 0.5
    far = jax.random.uniform(third, (size, size), jnp.float32, 0.3, 0.5)
    far = (far + far.T) * 0.5
    index = jnp.arange(size, dtype=jnp.int32)
    gap = jnp.abs(index[:, None] - index[None, :])
    return jnp.where(gap == 1, dense - near, jnp.where(gap == stride, dense - far, dense))


def draw_carried_block(key, part):
    return stencil_block(jax.random.fold_in(key, 11), B, TILE, 4.5, 6.5)


def draw_next_block(key, part):
    return stencil_block(jax.random.fold_in(key, 23), B, TILE, 4.5, 6.5)


def draw_tip_block(key, part):
    return symmetric_block(jax.random.fold_in(key, 37), NF, 1.0, 2.0)


def draw_coupling_values(key, part):
    first = jax.random.fold_in(jax.random.fold_in(key, 41), 0)
    shape = (B, NNZB * TILE)
    return jax.random.uniform(first, shape, jnp.float32, -0.15, 0.15)


def draw_block_cols(key, part):
    reach = NB // 4
    keys = jax.random.split(jax.random.fold_in(key, 5), NB)
    picks = jax.vmap(lambda single: jax.random.permutation(single, 2 * reach)[:NNZB - 1])(keys)
    offsets = picks.astype(jnp.int32) - reach
    offsets = jnp.where(offsets >= 0, offsets + 1, offsets)
    row_index = jnp.arange(NB, dtype=jnp.int32)[:, None]
    others = (row_index + offsets) % NB
    return jnp.concatenate([row_index, others], axis=1).astype(jnp.int32)


def block_scale(own_key, shape, cuts, smallest, top_value):
    gain, own = 1.0, jax.random.fold_in(own_key, 6)
    for axis_at, shards_of in cuts:
        draws = jnp.exp(jax.random.uniform(jax.random.fold_in(own, axis_at), (shards_of,), jnp.float32, smallest / len(cuts), top_value / len(cuts)))
        gain = gain * jnp.repeat(draws, shape[axis_at] // shards_of).reshape([-1 if axis == axis_at else 1 for axis in range(len(shape))])
    return gain


def scatter_about(stream_key, dims, scale, most, cuts=(), kind=jnp.bfloat16):
    array = scale * jax.random.normal(stream_key, dims, jnp.float32)
    if cuts:
        array = array * block_scale(stream_key, dims, cuts, -0.22, 0.18)
    return jnp.clip(array, -most, most).astype(kind)


def setup_inputs(seed: int = 0, part: int = 0) -> dict:
    streams_of = jax.random.split(jax.random.key(seed), 8)
    part_splits = jax.random.split(jax.random.fold_in(streams_of[7], part), 8)
    return {
        "carried_block": draw_carried_block(jax.random.fold_in(jax.random.fold_in(streams_of[7], part), 71), part),
        "coupling_values": draw_coupling_values(jax.random.fold_in(jax.random.fold_in(streams_of[7], part), 71), part),
        "block_cols": draw_block_cols(jax.random.fold_in(streams_of[7], 71), part),
        "next_block": draw_next_block(jax.random.fold_in(jax.random.fold_in(streams_of[7], part), 71), part),
        "fixed_rows": scatter_about(part_splits[4], (NF, B), 0.03, 0.1875, ((1, 16),), jnp.float32),
        "fixed_next": scatter_about(part_splits[5], (NF, B), 1.0, 6.0, ((1, 16),), jnp.float32),
        "tip_block": draw_tip_block(jax.random.fold_in(jax.random.fold_in(streams_of[7], part), 71), part),
    }


def matmul(left, right):
    return jnp.dot(left.astype(jnp.float32), right.astype(jnp.float32), precision=lax.Precision.HIGHEST, preferred_element_type=jnp.float32)

def assemble(block_cols, values):
    block_rows, nonzero = block_cols.shape
    width = values.shape[1] // nonzero
    columns = jnp.arange(NB, dtype=jnp.int32)
    onehot = (block_cols[:, :, None] == columns[None, None, :]).astype(values.dtype)
    shaped = values.reshape(block_rows, width, nonzero, width)
    dense = jnp.einsum('bsn,btsc->btnc', onehot, shaped, precision=lax.Precision.HIGHEST)
    return dense.reshape(block_rows * width, NB * width)

def reference(carried_block, coupling_values, block_cols, next_block, fixed_rows, fixed_next, tip_block):
    local_rows = B // N_ROW
    state = carried_block
    coupled = assemble(block_cols, coupling_values)
    carried = next_block
    fixed = fixed_rows
    fixed_carry = fixed_next
    tip = tip_block
    index = jnp.arange(B, dtype=jnp.int32)
    for panel in range(PANELS):
        begin = panel * local_rows
        finish = begin + local_rows
        tile = jnp.linalg.cholesky(state[begin:finish, begin:finish])
        solved = jax.scipy.linalg.solve_triangular(tile, state[:, begin:finish].T, lower=True)
        solved = jnp.where(index[None, :] >= finish, solved, 0.0)
        solved = solved.at[:, begin:finish].set(tile.T)
        coupled_t = jax.scipy.linalg.solve_triangular(tile, coupled[:, begin:finish].T, lower=True)
        fixed_panel = jax.scipy.linalg.solve_triangular(tile, fixed[:, begin:finish].T, lower=True).T
        below = (index >= finish)[:, None]
        state = state - jnp.where(below, matmul(solved.T, solved), 0.0)
        state = state.at[:, begin:finish].set(solved.T)
        state = state.at[begin:finish, finish:].set(0.0)
        coupled = coupled - matmul(coupled_t.T, solved)
        coupled = coupled.at[:, begin:finish].set(coupled_t.T)
        carried = carried - matmul(coupled_t.T, coupled_t)
        fixed = fixed - matmul(fixed_panel, solved)
        fixed = fixed.at[:, begin:finish].set(fixed_panel)
        fixed_carry = fixed_carry - matmul(fixed_panel, coupled_t)
        tip = tip - matmul(fixed_panel, fixed_panel.T)
    return (state, coupled, carried, fixed, fixed_carry, tip)
```

```python
import jax
import jax.numpy as jnp
from jax import lax
from jax.sharding import PartitionSpec as P

PANELS = 4
HIGHEST = lax.Precision.HIGHEST


def mdot(left, right):
    return jnp.dot(left, right, precision=HIGHEST, preferred_element_type=jnp.float32)


def tdot(left, right):
    return lax.dot_general(
        left, right, (((1,), (1,)), ((), ())), precision=HIGHEST, preferred_element_type=jnp.float32
    )


def assemble(block_cols, values, col_blocks):
    block_rows, nonzero = block_cols.shape
    width = values.shape[1] // nonzero
    span = col_blocks * width
    shaped = values.reshape(block_rows, width, nonzero, 1, width)
    shaped = jnp.broadcast_to(shaped, (block_rows, width, nonzero, col_blocks, width))
    shaped = shaped.reshape(block_rows, width, nonzero, span)
    lane_block = jnp.arange(span, dtype=jnp.int32) // width
    hit = block_cols[:, None, :, None] == lane_block[None, None, None, :]
    dense = jnp.where(hit, shaped, 0.0).sum(axis=2)
    return dense.reshape(block_rows * width, span)


def on_device(
    carried_block, coupling_values, block_cols, next_block, fixed_rows, fixed_next, tip_block
):
    rows, size = carried_block.shape
    width = coupling_values.shape[1] // block_cols.shape[1]
    factored = PANELS * rows
    me = lax.axis_index("row")
    is_top = me < PANELS
    top_at = jnp.minimum(me, PANELS - 1) * rows

    own_cols = carried_block[:, :factored]
    gathered_cols = lax.all_gather(own_cols, "row", axis=0, tiled=True)
    all_values = lax.all_gather(coupling_values, "row", axis=0, tiled=True)
    all_block_cols = lax.all_gather(block_cols, "row", axis=0, tiled=True)
    all_fixed = lax.all_gather(fixed_rows, "row", axis=1, tiled=True)

    head = gathered_cols[:factored]
    below = gathered_cols[factored:]
    head_factor = jnp.linalg.cholesky(head)
    head_inverse = jax.scipy.linalg.solve_triangular(
        head_factor, jnp.eye(factored, dtype=jnp.float32), lower=True
    )

    lower = tdot(own_cols, head_inverse)
    lower = jnp.where(is_top, lax.dynamic_slice_in_dim(head_factor, top_at, rows, 0), lower)
    lower_scaled = mdot(lower, head_inverse)
    state_rest = carried_block[:, factored:] - tdot(lower_scaled, below)
    state_rest = jnp.where(is_top, 0.0, state_rest)
    factor_state = jnp.concatenate([lower, state_rest], axis=1)

    coupled = assemble(block_cols, coupling_values, size // width)
    coupled_panel = tdot(coupled[:, :factored], head_inverse)
    coupled_scaled = mdot(coupled_panel, head_inverse)
    coupled_rest = coupled[:, factored:] - tdot(coupled_scaled, below)
    coupling_factor = jnp.concatenate([coupled_panel, coupled_rest], axis=1)

    head_blocks = factored // width
    block_rows, nonzero = all_block_cols.shape
    scaled_blocks = coupled_scaled.T.reshape(head_blocks, width, rows)
    scaled_blocks = jnp.concatenate(
        [scaled_blocks, jnp.zeros((1, width, rows), jnp.float32)], axis=0
    )
    picks = jnp.where(all_block_cols < head_blocks, all_block_cols, head_blocks)
    picked = jnp.take(scaled_blocks, picks, axis=0).reshape(block_rows, nonzero * width, rows)
    values_rows = all_values.reshape(block_rows, width, nonzero * width)
    carry = jnp.einsum(
        "rts,rsi->rti", values_rows, picked, precision=HIGHEST, preferred_element_type=jnp.float32
    )
    carried_next = next_block - carry.reshape(block_rows * width, rows).T

    fixed_panel = tdot(all_fixed[:, :factored], head_inverse)
    own_fixed_panel = lax.dynamic_slice_in_dim(fixed_panel, top_at, rows, 1)
    fixed_factor = jnp.where(is_top, own_fixed_panel, fixed_rows - tdot(fixed_panel, lower))
    fixed_carried = fixed_next - tdot(fixed_panel, coupled_panel)
    tip_next = tip_block - tdot(fixed_panel, fixed_panel)
    return (factor_state, coupling_factor, carried_next, fixed_factor, fixed_carried, tip_next)


def solution(mesh):
    return jax.shard_map(
        on_device,
        mesh=mesh,
        in_specs=(
            P(("hyper", "row"), None),
            P(("hyper", "row"), None),
            P("row", None),
            P(("hyper", "row"), None),
            P("hyper", "row"),
            P("hyper", "row"),
            P("hyper", None),
        ),
        out_specs=(
            P(("hyper", "row"), None),
            P(("hyper", "row"), None),
            P(("hyper", "row"), None),
            P("hyper", "row"),
            P("hyper", "row"),
            P("hyper", None),
        ),
        check_vma=False,
    )
```

```python
import jax
import jax.numpy as jnp
from jax import lax
from jax.sharding import PartitionSpec as P

PANELS = 4
BLOCK = 128
HIGHEST = lax.Precision.HIGHEST


def mdot(left, right):
    return jnp.dot(left, right, precision=HIGHEST, preferred_element_type=jnp.float32)


def tdot(left, right):
    return lax.dot_general(
        left, right, (((1,), (1,)), ((), ())), precision=HIGHEST, preferred_element_type=jnp.float32
    )


def assemble_t(block_cols, values, col_blocks):
    block_rows, nonzero = block_cols.shape
    width = values.shape[1] // nonzero
    span = block_rows * width
    flipped = values.T.reshape(nonzero, 1, width, span)
    spread = jnp.repeat(block_cols.T, width, axis=1)
    columns = jnp.arange(col_blocks, dtype=jnp.int32)
    hit = spread[:, None, None, :] == columns[None, :, None, None]
    dense = jnp.where(hit, flipped, 0.0).sum(axis=0)
    return dense.reshape(col_blocks * width, span)


def invert_lower(factor, block_inverses):
    inverses = jnp.stack(block_inverses)
    size = inverses.shape[1]
    while inverses.shape[0] > 1:
        pairs = inverses.shape[0] // 2
        first, second = inverses[0::2], inverses[1::2]
        coupling = jnp.stack(
            [
                factor[(2 * q + 1) * size:(2 * q + 2) * size, 2 * q * size:(2 * q + 1) * size]
                for q in range(pairs)
            ]
        )
        corner = jnp.einsum("qij,qjk->qik", second, coupling, precision=HIGHEST)
        corner = -jnp.einsum("qik,qkl->qil", corner, first, precision=HIGHEST)
        top = jnp.concatenate([first, jnp.zeros_like(first)], axis=2)
        bottom = jnp.concatenate([corner, second], axis=2)
        inverses = jnp.concatenate([top, bottom], axis=1)
        size *= 2
    return inverses[0]


def on_device(
    carried_block, coupling_values, block_cols, next_block, fixed_rows, fixed_next, tip_block
):
    rows, size = carried_block.shape
    value_rows, value_cols = coupling_values.shape
    local_block_rows, nonzero = block_cols.shape
    width = value_cols // nonzero
    fixed_count = fixed_rows.shape[0]
    factored = PANELS * rows
    me = lax.axis_index("row")
    is_top = me < PANELS
    top_at = jnp.minimum(me, PANELS - 1) * rows
    fixed_cols = fixed_rows.shape[1]
    block = min(BLOCK, rows)
    cols_count = local_block_rows * nonzero
    lanes = max(value_cols, fixed_cols, cols_count)

    def widen(part):
        return jnp.pad(part, ((0, 0), (0, lanes - part.shape[1])))

    cols_row = block_cols.reshape(1, cols_count).astype(jnp.float32)
    packed = jnp.concatenate([widen(coupling_values), widen(fixed_rows), widen(cols_row)], axis=0)
    pad = (-packed.shape[0]) % 8
    packed = jnp.concatenate([packed, jnp.zeros((pad, lanes), jnp.float32)], axis=0)
    gathered = lax.all_gather(packed, "row", axis=0)
    devices = gathered.shape[0]
    all_values = gathered[:, :value_rows, :value_cols].reshape(devices * value_rows, value_cols)
    all_fixed = gathered[:, value_rows:value_rows + fixed_count, :fixed_cols].transpose(1, 0, 2)
    all_fixed = all_fixed.reshape(fixed_count, devices * fixed_cols)
    all_block_cols = gathered[:, value_rows + fixed_count, :cols_count]
    all_block_cols = jnp.round(all_block_cols).astype(jnp.int32).reshape(-1, nonzero)

    chunks = [
        lax.all_gather(carried_block[:, c * rows:(c + 1) * rows], "row", axis=0, tiled=True)
        for c in range(PANELS)
    ]

    columns = []
    block_inverses = []
    for k in range(factored // block):
        chunk, offset = divmod(k * block, rows)
        panel = chunks[chunk][k * block:factored, offset:offset + block]
        if k:
            done = jnp.concatenate([col[k * block:] for col in columns], axis=1)
            panel = panel - tdot(done, done[:block])
        diagonal = jnp.linalg.cholesky(panel[:block])
        diagonal_inverse = jax.scipy.linalg.solve_triangular(
            diagonal, jnp.eye(block, dtype=jnp.float32), lower=True
        )
        under = tdot(panel[block:], diagonal_inverse)
        column = jnp.concatenate(
            [jnp.zeros((k * block, block), jnp.float32), diagonal, under], axis=0
        )
        columns.append(column)
        block_inverses.append(diagonal_inverse)
    head_factor = jnp.concatenate(columns, axis=1)
    head_inverse = invert_lower(head_factor, block_inverses)

    def minus_below(scaled):
        total = None
        for c in range(PANELS):
            part = tdot(scaled[:, c * rows:(c + 1) * rows], chunks[c][factored:])
            total = part if total is None else total + part
        return total

    own_cols = carried_block[:, :factored]
    lower = tdot(own_cols, head_inverse)
    lower = jnp.where(is_top, lax.dynamic_slice_in_dim(head_factor, top_at, rows, 0), lower)
    lower_scaled = mdot(lower, head_inverse)
    state_rest = carried_block[:, factored:] - minus_below(lower_scaled)
    state_rest = jnp.where(is_top, 0.0, state_rest)
    factor_state = jnp.concatenate([lower, state_rest], axis=1)

    coupled = assemble_t(block_cols, coupling_values, size // width).T
    coupled_panel = tdot(coupled[:, :factored], head_inverse)
    coupled_scaled = mdot(coupled_panel, head_inverse)
    coupled_rest = coupled[:, factored:] - minus_below(coupled_scaled)
    coupling_factor = jnp.concatenate([coupled_panel, coupled_rest], axis=1)

    coupling_head_t = assemble_t(all_block_cols, all_values, factored // width)
    carried_next = next_block - mdot(coupled_scaled, coupling_head_t)

    fixed_panel = tdot(all_fixed[:, :factored], head_inverse)
    own_fixed_panel = lax.dynamic_slice_in_dim(fixed_panel, top_at, rows, 1)
    fixed_factor = jnp.where(is_top, own_fixed_panel, fixed_rows - tdot(fixed_panel, lower))
    fixed_carried = fixed_next - tdot(fixed_panel, coupled_panel)
    tip_next = tip_block - tdot(fixed_panel, fixed_panel)
    return (factor_state, coupling_factor, carried_next, fixed_factor, fixed_carried, tip_next)


def solution(mesh):
    return jax.shard_map(
        on_device,
        mesh=mesh,
        in_specs=(
            P(("hyper", "row"), None),
            P(("hyper", "row"), None),
            P("row", None),
            P(("hyper", "row"), None),
            P("hyper", "row"),
            P("hyper", "row"),
            P("hyper", None),
        ),
        out_specs=(
            P(("hyper", "row"), None),
            P(("hyper", "row"), None),
            P(("hyper", "row"), None),
            P("hyper", "row"),
            P("hyper", "row"),
            P("hyper", None),
        ),
        check_vma=False,
    )
```

```python
import jax
import jax.numpy as jnp
from jax import lax
from jax.sharding import PartitionSpec as P

PANELS = 4
BLOCK = 128
HIGHEST = lax.Precision.HIGHEST
HIGH = lax.Precision.HIGH


def mdot(left, right, precision=HIGHEST):
    return jnp.dot(left, right, precision=precision, preferred_element_type=jnp.float32)


def tdot(left, right, precision=HIGHEST):
    return lax.dot_general(
        left, right, (((1,), (1,)), ((), ())), precision=precision, preferred_element_type=jnp.float32
    )


def assemble_t(block_cols, values, col_blocks):
    block_rows, nonzero = block_cols.shape
    width = values.shape[1] // nonzero
    span = block_rows * width
    flipped = values.T.reshape(nonzero, 1, width, span)
    spread = jnp.repeat(block_cols.T, width, axis=1)
    columns = jnp.arange(col_blocks, dtype=jnp.int32)
    hit = spread[:, None, None, :] == columns[None, :, None, None]
    dense = jnp.where(hit, flipped, 0.0).sum(axis=0)
    return dense.reshape(col_blocks * width, span)


def invert_lower(factor, block_inverses):
    inverses = jnp.stack(block_inverses)
    size = inverses.shape[1]
    while inverses.shape[0] > 1:
        pairs = inverses.shape[0] // 2
        first, second = inverses[0::2], inverses[1::2]
        coupling = jnp.stack(
            [
                factor[(2 * q + 1) * size:(2 * q + 2) * size, 2 * q * size:(2 * q + 1) * size]
                for q in range(pairs)
            ]
        )
        corner = jnp.einsum("qij,qjk->qik", second, coupling, precision=HIGHEST)
        corner = -jnp.einsum("qik,qkl->qil", corner, first, precision=HIGHEST)
        top = jnp.concatenate([first, jnp.zeros_like(first)], axis=2)
        bottom = jnp.concatenate([corner, second], axis=2)
        inverses = jnp.concatenate([top, bottom], axis=1)
        size *= 2
    return inverses[0]


def on_device(
    carried_block, coupling_values, block_cols, next_block, fixed_rows, fixed_next, tip_block
):
    rows, size = carried_block.shape
    value_rows, value_cols = coupling_values.shape
    local_block_rows, nonzero = block_cols.shape
    width = value_cols // nonzero
    fixed_count = fixed_rows.shape[0]
    factored = PANELS * rows
    me = lax.axis_index("row")
    is_top = me < PANELS
    top_at = jnp.minimum(me, PANELS - 1) * rows
    fixed_cols = fixed_rows.shape[1]
    block = min(BLOCK, rows)
    cols_count = local_block_rows * nonzero
    lanes = max(value_cols, fixed_cols, cols_count)

    def widen(part):
        return jnp.pad(part, ((0, 0), (0, lanes - part.shape[1])))

    cols_row = block_cols.reshape(1, cols_count).astype(jnp.float32)
    packed = jnp.concatenate([widen(coupling_values), widen(fixed_rows), widen(cols_row)], axis=0)
    pad = (-packed.shape[0]) % 8
    packed = jnp.concatenate([packed, jnp.zeros((pad, lanes), jnp.float32)], axis=0)
    gathered = lax.all_gather(packed, "row", axis=0)
    devices = gathered.shape[0]
    all_values = gathered[:, :value_rows, :value_cols].reshape(devices * value_rows, value_cols)
    all_fixed = gathered[:, value_rows:value_rows + fixed_count, :fixed_cols].transpose(1, 0, 2)
    all_fixed = all_fixed.reshape(fixed_count, devices * fixed_cols)
    all_block_cols = gathered[:, value_rows + fixed_count, :cols_count]
    all_block_cols = jnp.round(all_block_cols).astype(jnp.int32).reshape(-1, nonzero)

    blocks = factored // block
    widths = [1]
    while sum(widths) < blocks:
        widths.append(min(sum(widths), blocks - sum(widths)))
    bounds = [0]
    for count in widths:
        bounds.append(bounds[-1] + count * block)
    chunks = [
        lax.all_gather(carried_block[:, lo:hi], "row", axis=0, tiled=True)
        for lo, hi in zip(bounds[:-1], bounds[1:])
    ]
    chunk_of = [c for c, count in enumerate(widths) for _ in range(count)]

    columns = []
    block_inverses = []
    for k in range(factored // block):
        chunk = chunk_of[k]
        offset = k * block - bounds[chunk]
        panel = chunks[chunk][k * block:factored, offset:offset + block]
        if k:
            done = jnp.concatenate([col[k * block:] for col in columns], axis=1)
            panel = panel - tdot(done, done[:block])
        diagonal = jnp.linalg.cholesky(panel[:block])
        diagonal_inverse = jax.scipy.linalg.solve_triangular(
            diagonal, jnp.eye(block, dtype=jnp.float32), lower=True
        )
        under = tdot(panel[block:], diagonal_inverse)
        column = jnp.concatenate(
            [jnp.zeros((k * block, block), jnp.float32), diagonal, under], axis=0
        )
        columns.append(column)
        block_inverses.append(diagonal_inverse)
    head_factor = jnp.concatenate(columns, axis=1)
    head_inverse = invert_lower(head_factor, block_inverses)

    def minus_below(scaled):
        total = None
        for c, (lo, hi) in enumerate(zip(bounds[:-1], bounds[1:])):
            part = tdot(scaled[:, lo:hi], chunks[c][factored:], HIGH)
            total = part if total is None else total + part
        return total

    own_cols = carried_block[:, :factored]
    lower = tdot(own_cols, head_inverse, HIGH)
    lower = jnp.where(is_top, lax.dynamic_slice_in_dim(head_factor, top_at, rows, 0), lower)
    lower_scaled = mdot(lower, head_inverse, HIGH)
    state_rest = carried_block[:, factored:] - minus_below(lower_scaled)
    state_rest = jnp.where(is_top, 0.0, state_rest)
    factor_state = jnp.concatenate([lower, state_rest], axis=1)

    coupled = assemble_t(block_cols, coupling_values, size // width).T
    coupled_panel = tdot(coupled[:, :factored], head_inverse, HIGH)
    coupled_scaled = mdot(coupled_panel, head_inverse, HIGH)
    coupled_rest = coupled[:, factored:] - minus_below(coupled_scaled)
    coupling_factor = jnp.concatenate([coupled_panel, coupled_rest], axis=1)

    coupling_head_t = assemble_t(all_block_cols, all_values, factored // width)
    carried_next = next_block - mdot(coupled_scaled, coupling_head_t, HIGH)

    fixed_panel = tdot(all_fixed[:, :factored], head_inverse)
    own_fixed_panel = lax.dynamic_slice_in_dim(fixed_panel, top_at, rows, 1)
    fixed_factor = jnp.where(is_top, own_fixed_panel, fixed_rows - tdot(fixed_panel, lower))
    fixed_carried = fixed_next - tdot(fixed_panel, coupled_panel)
    tip_next = tip_block - tdot(fixed_panel, fixed_panel)
    return (factor_state, coupling_factor, carried_next, fixed_factor, fixed_carried, tip_next)


def solution(mesh):
    return jax.shard_map(
        on_device,
        mesh=mesh,
        in_specs=(
            P(("hyper", "row"), None),
            P(("hyper", "row"), None),
            P("row", None),
            P(("hyper", "row"), None),
            P("hyper", "row"),
            P("hyper", "row"),
            P("hyper", None),
        ),
        out_specs=(
            P(("hyper", "row"), None),
            P(("hyper", "row"), None),
            P(("hyper", "row"), None),
            P("hyper", "row"),
            P("hyper", "row"),
            P("hyper", None),
        ),
        check_vma=False,
    )
```

```python
import jax
import jax.numpy as jnp
from jax import lax
from jax.sharding import PartitionSpec as P

PANELS = 4
BLOCK = 128
HIGHEST = lax.Precision.HIGHEST
HIGH = lax.Precision.HIGH


def mdot(left, right, precision=HIGHEST):
    return jnp.dot(left, right, precision=precision, preferred_element_type=jnp.float32)


def tdot(left, right, precision=HIGHEST):
    return lax.dot_general(
        left, right, (((1,), (1,)), ((), ())), precision=precision, preferred_element_type=jnp.float32
    )


def assemble_t(block_cols, values_t, col_blocks):
    block_rows, nonzero = block_cols.shape
    width = values_t.shape[0] // nonzero
    span = block_rows * width
    flipped = values_t.reshape(nonzero, 1, width, span)
    spread = jnp.repeat(block_cols.T, width, axis=1)
    columns = jnp.arange(col_blocks, dtype=jnp.int32)
    hit = spread[:, None, None, :] == columns[None, :, None, None]
    dense = jnp.where(hit, flipped, 0.0).sum(axis=0)
    return dense.reshape(col_blocks * width, span)


def invert_lower(factor, block_inverses):
    inverses = jnp.stack(block_inverses)
    size = inverses.shape[1]
    while inverses.shape[0] > 1:
        pairs = inverses.shape[0] // 2
        first, second = inverses[0::2], inverses[1::2]
        coupling = jnp.stack(
            [
                factor[(2 * q + 1) * size:(2 * q + 2) * size, 2 * q * size:(2 * q + 1) * size]
                for q in range(pairs)
            ]
        )
        corner = jnp.einsum("qij,qjk->qik", second, coupling, precision=HIGHEST)
        corner = -jnp.einsum("qik,qkl->qil", corner, first, precision=HIGHEST)
        top = jnp.concatenate([first, jnp.zeros_like(first)], axis=2)
        bottom = jnp.concatenate([corner, second], axis=2)
        inverses = jnp.concatenate([top, bottom], axis=1)
        size *= 2
    return inverses[0]


def on_device(
    carried_block, coupling_values, block_cols, next_block, fixed_rows, fixed_next, tip_block
):
    rows, size = carried_block.shape
    value_rows, value_cols = coupling_values.shape
    local_block_rows, nonzero = block_cols.shape
    width = value_cols // nonzero
    fixed_count = fixed_rows.shape[0]
    factored = PANELS * rows
    me = lax.axis_index("row")
    is_top = me < PANELS
    top_at = jnp.minimum(me, PANELS - 1) * rows
    fixed_cols = fixed_rows.shape[1]
    block = min(BLOCK, rows)
    cols_count = local_block_rows * nonzero
    lanes = max(value_cols, fixed_cols, cols_count)

    def widen(part):
        return jnp.pad(part, ((0, 0), (0, lanes - part.shape[1])))

    values_t = coupling_values.T
    cols_row = block_cols.reshape(1, cols_count).astype(jnp.float32)
    packed = jnp.concatenate([widen(fixed_rows), widen(cols_row)], axis=0)
    pad = (-packed.shape[0]) % 8
    packed = jnp.concatenate([packed, jnp.zeros((pad, lanes), jnp.float32)], axis=0)
    gathered = lax.all_gather(packed, "row", axis=0)
    devices = gathered.shape[0]
    all_fixed = gathered[:, :fixed_count, :fixed_cols].transpose(1, 0, 2)
    all_fixed = all_fixed.reshape(fixed_count, devices * fixed_cols)
    all_block_cols = gathered[:, fixed_count, :cols_count]
    all_block_cols = jnp.round(all_block_cols).astype(jnp.int32).reshape(-1, nonzero)

    blocks = factored // block
    widths = [rows // block] * PANELS
    bounds = [0]
    for count in widths:
        bounds.append(bounds[-1] + count * block)
    chunks = [
        lax.all_gather(carried_block[:, lo:hi], "row", axis=0, tiled=True)
        for lo, hi in zip(bounds[:-1], bounds[1:])
    ]
    chunk_of = [c for c, count in enumerate(widths) for _ in range(count)]

    columns = []
    block_inverses = []
    for k in range(factored // block):
        chunk = chunk_of[k]
        offset = k * block - bounds[chunk]
        panel = chunks[chunk][k * block:factored, offset:offset + block]
        if k:
            done = jnp.concatenate([col[k * block:] for col in columns], axis=1)
            panel = panel - tdot(done, done[:block])
        diagonal = jnp.linalg.cholesky(panel[:block], symmetrize_input=False)
        diagonal_inverse = jax.scipy.linalg.solve_triangular(
            diagonal, jnp.eye(block, dtype=jnp.float32), lower=True
        )
        under = tdot(panel[block:], diagonal_inverse)
        column = jnp.concatenate(
            [jnp.zeros((k * block, block), jnp.float32), diagonal, under], axis=0
        )
        columns.append(column)
        block_inverses.append(diagonal_inverse)
    head_factor = jnp.concatenate(columns, axis=1)
    head_inverse = invert_lower(head_factor, block_inverses)

    def minus_below(scaled):
        total = None
        for c, (lo, hi) in enumerate(zip(bounds[:-1], bounds[1:])):
            part = tdot(scaled[:, lo:hi], chunks[c][factored:], HIGH)
            total = part if total is None else total + part
        return total

    own_cols = carried_block[:, :factored]
    lower = tdot(own_cols, head_inverse, HIGH)
    lower = jnp.where(is_top, lax.dynamic_slice_in_dim(head_factor, top_at, rows, 0), lower)
    lower_scaled = mdot(lower, head_inverse, HIGH)
    state_rest = carried_block[:, factored:] - minus_below(lower_scaled)
    state_rest = jnp.where(is_top, 0.0, state_rest)
    factor_state = jnp.concatenate([lower, state_rest], axis=1)

    coupled = assemble_t(block_cols, values_t, size // width).T
    coupled_panel = tdot(coupled[:, :factored], head_inverse, HIGH)
    coupled_scaled = mdot(coupled_panel, head_inverse, HIGH)
    coupled_rest = coupled[:, factored:] - minus_below(coupled_scaled)
    coupling_factor = jnp.concatenate([coupled_panel, coupled_rest], axis=1)

    all_values_t = lax.all_gather(values_t, "row", axis=1, tiled=True)
    coupling_head_t = assemble_t(all_block_cols, all_values_t, factored // width)
    carried_next = next_block - mdot(coupled_scaled, coupling_head_t, HIGH)

    fixed_panel = tdot(all_fixed[:, :factored], head_inverse)
    own_fixed_panel = lax.dynamic_slice_in_dim(fixed_panel, top_at, rows, 1)
    fixed_factor = jnp.where(is_top, own_fixed_panel, fixed_rows - tdot(fixed_panel, lower))
    fixed_carried = fixed_next - tdot(fixed_panel, coupled_panel)
    tip_next = tip_block - tdot(fixed_panel, fixed_panel)
    return (factor_state, coupling_factor, carried_next, fixed_factor, fixed_carried, tip_next)


def solution(mesh):
    return jax.shard_map(
        on_device,
        mesh=mesh,
        in_specs=(
            P(("hyper", "row"), None),
            P(("hyper", "row"), None),
            P("row", None),
            P(("hyper", "row"), None),
            P("hyper", "row"),
            P("hyper", "row"),
            P("hyper", None),
        ),
        out_specs=(
            P(("hyper", "row"), None),
            P(("hyper", "row"), None),
            P(("hyper", "row"), None),
            P("hyper", "row"),
            P("hyper", "row"),
            P("hyper", None),
        ),
        check_vma=False,
    )
```

```python
import jax
import jax.numpy as jnp
from jax import lax
from jax.sharding import PartitionSpec as P

PANELS = 4
BLOCK = 128
REACH = 32
HIGHEST = lax.Precision.HIGHEST
HIGH = lax.Precision.HIGH


def mdot(left, right, precision=HIGHEST):
    return jnp.dot(left, right, precision=precision, preferred_element_type=jnp.float32)


def tdot(left, right, precision=HIGHEST):
    return lax.dot_general(
        left, right, (((1,), (1,)), ((), ())), precision=precision, preferred_element_type=jnp.float32
    )


def assemble_t(block_cols, values_t, col_blocks):
    block_rows, nonzero = block_cols.shape
    width = values_t.shape[0] // nonzero
    span = block_rows * width
    flipped = values_t.reshape(nonzero, 1, width, span)
    spread = jnp.repeat(block_cols.T, width, axis=1)
    columns = jnp.arange(col_blocks, dtype=jnp.int32)
    hit = spread[:, None, None, :] == columns[None, :, None, None]
    dense = jnp.where(hit, flipped, 0.0).sum(axis=0)
    return dense.reshape(col_blocks * width, span)


def invert_lower(factor, block_inverses):
    inverses = jnp.stack(block_inverses)
    size = inverses.shape[1]
    while inverses.shape[0] > 1:
        pairs = inverses.shape[0] // 2
        first, second = inverses[0::2], inverses[1::2]
        coupling = jnp.stack(
            [
                factor[(2 * q + 1) * size:(2 * q + 2) * size, 2 * q * size:(2 * q + 1) * size]
                for q in range(pairs)
            ]
        )
        corner = jnp.einsum("qij,qjk->qik", second, coupling, precision=HIGHEST)
        corner = -jnp.einsum("qik,qkl->qil", corner, first, precision=HIGHEST)
        top = jnp.concatenate([first, jnp.zeros_like(first)], axis=2)
        bottom = jnp.concatenate([corner, second], axis=2)
        inverses = jnp.concatenate([top, bottom], axis=1)
        size *= 2
    return inverses[0]


def on_device(
    carried_block, coupling_values, block_cols, next_block, fixed_rows, fixed_next, tip_block
):
    rows, size = carried_block.shape
    value_rows, value_cols = coupling_values.shape
    local_block_rows, nonzero = block_cols.shape
    width = value_cols // nonzero
    fixed_count = fixed_rows.shape[0]
    factored = PANELS * rows
    me = lax.axis_index("row")
    is_top = me < PANELS
    top_at = jnp.minimum(me, PANELS - 1) * rows
    fixed_cols = fixed_rows.shape[1]
    block = min(BLOCK, rows)
    cols_count = local_block_rows * nonzero
    lanes = max(value_cols, fixed_cols, cols_count)

    def widen(part):
        return jnp.pad(part, ((0, 0), (0, lanes - part.shape[1])))

    values_t = coupling_values.T
    cols_row = block_cols.reshape(1, cols_count).astype(jnp.float32)
    packed = jnp.concatenate([widen(fixed_rows), widen(cols_row)], axis=0)
    pad = (-packed.shape[0]) % 8
    packed = jnp.concatenate([packed, jnp.zeros((pad, lanes), jnp.float32)], axis=0)
    gathered = lax.all_gather(packed, "row", axis=0)
    devices = gathered.shape[0]
    all_fixed = gathered[:, :fixed_count, :fixed_cols].transpose(1, 0, 2)
    all_fixed = all_fixed.reshape(fixed_count, devices * fixed_cols)
    all_block_cols = gathered[:, fixed_count, :cols_count]
    all_block_cols = jnp.round(all_block_cols).astype(jnp.int32).reshape(-1, nonzero)

    blocks = factored // block
    widths = [rows // block] * PANELS
    bounds = [0]
    for count in widths:
        bounds.append(bounds[-1] + count * block)
    chunks = [
        lax.all_gather(carried_block[:, lo:hi], "row", axis=0, tiled=True)
        for lo, hi in zip(bounds[:-1], bounds[1:])
    ]
    chunk_of = [c for c, count in enumerate(widths) for _ in range(count)]

    columns = []
    block_inverses = []
    for k in range(factored // block):
        chunk = chunk_of[k]
        offset = k * block - bounds[chunk]
        panel = chunks[chunk][k * block:factored, offset:offset + block]
        if k:
            done = jnp.concatenate([col[k * block:] for col in columns], axis=1)
            panel = panel - tdot(done, done[:block])
        diagonal = jnp.linalg.cholesky(panel[:block], symmetrize_input=False)
        diagonal_inverse = jax.scipy.linalg.solve_triangular(
            diagonal, jnp.eye(block, dtype=jnp.float32), lower=True
        )
        under = tdot(panel[block:], diagonal_inverse)
        column = jnp.concatenate(
            [jnp.zeros((k * block, block), jnp.float32), diagonal, under], axis=0
        )
        columns.append(column)
        block_inverses.append(diagonal_inverse)
    head_factor = jnp.concatenate(columns, axis=1)
    head_inverse = invert_lower(head_factor, block_inverses)

    def minus_below(scaled):
        total = None
        for c, (lo, hi) in enumerate(zip(bounds[:-1], bounds[1:])):
            part = tdot(scaled[:, lo:hi], chunks[c][factored:], HIGH)
            total = part if total is None else total + part
        return total

    own_cols = carried_block[:, :factored]
    lower = tdot(own_cols, head_inverse, HIGH)
    lower = jnp.where(is_top, lax.dynamic_slice_in_dim(head_factor, top_at, rows, 0), lower)
    lower_scaled = mdot(lower, head_inverse, HIGH)
    state_rest = carried_block[:, factored:] - minus_below(lower_scaled)
    state_rest = jnp.where(is_top, 0.0, state_rest)
    factor_state = jnp.concatenate([lower, state_rest], axis=1)

    coupled = assemble_t(block_cols, values_t, size // width).T
    coupled_panel = tdot(coupled[:, :factored], head_inverse, HIGH)
    coupled_scaled = mdot(coupled_panel, head_inverse, HIGH)
    coupled_rest = coupled[:, factored:] - minus_below(coupled_scaled)
    coupling_factor = jnp.concatenate([coupled_panel, coupled_rest], axis=1)

    all_values_t = lax.all_gather(values_t, "row", axis=1, tiled=True)
    all_blocks = size // width
    head_blocks = factored // width
    near_end = min(head_blocks + REACH, all_blocks)
    far_start = max(all_blocks - REACH, near_end)
    spans = [(lo, hi) for lo, hi in ((0, near_end), (far_start, all_blocks)) if hi > lo]
    pieces = []
    at = 0
    for lo, hi in spans:
        if lo > at:
            pieces.append(next_block[:, at * width:lo * width])
        head_t = assemble_t(all_block_cols[lo:hi], all_values_t[:, lo * width:hi * width], head_blocks)
        pieces.append(
            next_block[:, lo * width:hi * width] - mdot(coupled_scaled, head_t, HIGH)
        )
        at = hi
    if at < all_blocks:
        pieces.append(next_block[:, at * width:])
    carried_next = jnp.concatenate(pieces, axis=1)

    fixed_panel = tdot(all_fixed[:, :factored], head_inverse)
    own_fixed_panel = lax.dynamic_slice_in_dim(fixed_panel, top_at, rows, 1)
    fixed_factor = jnp.where(is_top, own_fixed_panel, fixed_rows - tdot(fixed_panel, lower))
    fixed_carried = fixed_next - tdot(fixed_panel, coupled_panel)
    tip_next = tip_block - tdot(fixed_panel, fixed_panel)
    return (factor_state, coupling_factor, carried_next, fixed_factor, fixed_carried, tip_next)


def solution(mesh):
    return jax.shard_map(
        on_device,
        mesh=mesh,
        in_specs=(
            P(("hyper", "row"), None),
            P(("hyper", "row"), None),
            P("row", None),
            P(("hyper", "row"), None),
            P("hyper", "row"),
            P("hyper", "row"),
            P("hyper", None),
        ),
        out_specs=(
            P(("hyper", "row"), None),
            P(("hyper", "row"), None),
            P(("hyper", "row"), None),
            P("hyper", "row"),
            P("hyper", "row"),
            P("hyper", None),
        ),
        check_vma=False,
    )
```

```python
import jax
import jax.numpy as jnp
from jax import lax
from jax.sharding import PartitionSpec as P

PANELS = 4
BLOCK = 128
REACH = 32
HIGHEST = lax.Precision.HIGHEST
HIGH = lax.Precision.HIGH


def mdot(left, right, precision=HIGHEST):
    return jnp.dot(left, right, precision=precision, preferred_element_type=jnp.float32)


def tdot(left, right, precision=HIGHEST):
    return lax.dot_general(
        left, right, (((1,), (1,)), ((), ())), precision=precision, preferred_element_type=jnp.float32
    )


def assemble_t(block_cols, values_t, col_blocks):
    block_rows, nonzero = block_cols.shape
    width = values_t.shape[0] // nonzero
    span = block_rows * width
    flipped = values_t.reshape(nonzero, 1, width, span)
    spread = jnp.repeat(block_cols.T, width, axis=1)
    columns = jnp.arange(col_blocks, dtype=jnp.int32)
    hit = spread[:, None, None, :] == columns[None, :, None, None]
    dense = jnp.where(hit, flipped, 0.0).sum(axis=0)
    return dense.reshape(col_blocks * width, span)


def invert_lower(factor, block_inverses):
    inverses = jnp.stack(block_inverses)
    size = inverses.shape[1]
    while inverses.shape[0] > 1:
        pairs = inverses.shape[0] // 2
        first, second = inverses[0::2], inverses[1::2]
        coupling = jnp.stack(
            [
                factor[(2 * q + 1) * size:(2 * q + 2) * size, 2 * q * size:(2 * q + 1) * size]
                for q in range(pairs)
            ]
        )
        corner = jnp.einsum("qij,qjk->qik", second, coupling, precision=HIGHEST)
        corner = -jnp.einsum("qik,qkl->qil", corner, first, precision=HIGHEST)
        top = jnp.concatenate([first, jnp.zeros_like(first)], axis=2)
        bottom = jnp.concatenate([corner, second], axis=2)
        inverses = jnp.concatenate([top, bottom], axis=1)
        size *= 2
    return inverses[0]


def on_device(
    carried_block, coupling_values, block_cols, next_block, fixed_rows, fixed_next, tip_block
):
    rows, size = carried_block.shape
    value_rows, value_cols = coupling_values.shape
    local_block_rows, nonzero = block_cols.shape
    width = value_cols // nonzero
    fixed_count = fixed_rows.shape[0]
    factored = PANELS * rows
    me = lax.axis_index("row")
    is_top = me < PANELS
    top_at = jnp.minimum(me, PANELS - 1) * rows
    fixed_cols = fixed_rows.shape[1]
    block = min(BLOCK, rows)
    cols_count = local_block_rows * nonzero
    lanes = max(value_cols, fixed_cols, cols_count)

    def widen(part):
        return jnp.pad(part, ((0, 0), (0, lanes - part.shape[1])))

    values_t = coupling_values.T
    cols_row = block_cols.reshape(1, cols_count).astype(jnp.float32)
    packed = jnp.concatenate([widen(fixed_rows), widen(cols_row)], axis=0)
    pad = (-packed.shape[0]) % 8
    packed = jnp.concatenate([packed, jnp.zeros((pad, lanes), jnp.float32)], axis=0)
    gathered = lax.all_gather(packed, "row", axis=0)
    devices = gathered.shape[0]
    all_fixed = gathered[:, :fixed_count, :fixed_cols].transpose(1, 0, 2)
    all_fixed = all_fixed.reshape(fixed_count, devices * fixed_cols)
    all_block_cols = gathered[:, fixed_count, :cols_count]
    all_block_cols = jnp.round(all_block_cols).astype(jnp.int32).reshape(-1, nonzero)

    blocks = factored // block
    widths = [rows // block] * PANELS
    bounds = [0]
    for count in widths:
        bounds.append(bounds[-1] + count * block)
    chunks = [
        lax.all_gather(carried_block[:, lo:hi], "row", axis=0, tiled=True)
        for lo, hi in zip(bounds[:-1], bounds[1:])
    ]
    chunk_of = [c for c, count in enumerate(widths) for _ in range(count)]

    columns = []
    block_inverses = []
    for k in range(factored // block):
        chunk = chunk_of[k]
        offset = k * block - bounds[chunk]
        panel = chunks[chunk][k * block:factored, offset:offset + block]
        if k:
            done = jnp.concatenate([col[k * block:] for col in columns], axis=1)
            panel = panel - tdot(done, done[:block])
        diagonal = jnp.linalg.cholesky(panel[:block], symmetrize_input=False)
        diagonal_inverse = jax.scipy.linalg.solve_triangular(
            diagonal, jnp.eye(block, dtype=jnp.float32), lower=True
        )
        under = tdot(panel[block:], diagonal_inverse)
        column = jnp.concatenate(
            [jnp.zeros((k * block, block), jnp.float32), diagonal, under], axis=0
        )
        columns.append(column)
        block_inverses.append(diagonal_inverse)
    head_factor = jnp.concatenate(columns, axis=1)
    head_inverse = invert_lower(head_factor, block_inverses)

    def minus_below(scaled):
        total = None
        for c, (lo, hi) in enumerate(zip(bounds[:-1], bounds[1:])):
            part = tdot(scaled[:, lo:hi], chunks[c][factored:], HIGH)
            total = part if total is None else total + part
        return total

    coupled = assemble_t(block_cols, values_t, size // width).T
    stacked = jnp.concatenate([carried_block[:, :factored], coupled[:, :factored]], axis=0)
    panels = tdot(stacked, head_inverse, HIGH)
    lower = jnp.where(
        is_top, lax.dynamic_slice_in_dim(head_factor, top_at, rows, 0), panels[:rows]
    )
    coupled_panel = panels[rows:]
    scaled = mdot(jnp.concatenate([lower, coupled_panel], axis=0), head_inverse, HIGH)
    coupled_scaled = scaled[rows:]
    updates = minus_below(scaled)
    state_rest = jnp.where(is_top, 0.0, carried_block[:, factored:] - updates[:rows])
    factor_state = jnp.concatenate([lower, state_rest], axis=1)
    coupled_rest = coupled[:, factored:] - updates[rows:]
    coupling_factor = jnp.concatenate([coupled_panel, coupled_rest], axis=1)

    all_values_t = lax.all_gather(values_t, "row", axis=1, tiled=True)
    all_blocks = size // width
    head_blocks = factored // width
    near_end = min(head_blocks + REACH, all_blocks)
    far_start = max(all_blocks - REACH, near_end)
    spans = [(lo, hi) for lo, hi in ((0, near_end), (far_start, all_blocks)) if hi > lo]
    pieces = []
    at = 0
    for lo, hi in spans:
        if lo > at:
            pieces.append(next_block[:, at * width:lo * width])
        head_t = assemble_t(all_block_cols[lo:hi], all_values_t[:, lo * width:hi * width], head_blocks)
        pieces.append(
            next_block[:, lo * width:hi * width] - mdot(coupled_scaled, head_t, HIGH)
        )
        at = hi
    if at < all_blocks:
        pieces.append(next_block[:, at * width:])
    carried_next = jnp.concatenate(pieces, axis=1)

    fixed_panel = tdot(all_fixed[:, :factored], head_inverse)
    own_fixed_panel = lax.dynamic_slice_in_dim(fixed_panel, top_at, rows, 1)
    fixed_factor = jnp.where(is_top, own_fixed_panel, fixed_rows - tdot(fixed_panel, lower))
    fixed_carried = fixed_next - tdot(fixed_panel, coupled_panel)
    tip_next = tip_block - tdot(fixed_panel, fixed_panel)
    return (factor_state, coupling_factor, carried_next, fixed_factor, fixed_carried, tip_next)


def solution(mesh):
    return jax.shard_map(
        on_device,
        mesh=mesh,
        in_specs=(
            P(("hyper", "row"), None),
            P(("hyper", "row"), None),
            P("row", None),
            P(("hyper", "row"), None),
            P("hyper", "row"),
            P("hyper", "row"),
            P("hyper", None),
        ),
        out_specs=(
            P(("hyper", "row"), None),
            P(("hyper", "row"), None),
            P(("hyper", "row"), None),
            P("hyper", "row"),
            P("hyper", "row"),
            P("hyper", None),
        ),
        check_vma=False,
    )
```

```python
import jax
import jax.numpy as jnp
from jax import lax
from jax.sharding import PartitionSpec as P

PANELS = 4
BLOCK = 128
REACH = 32
HIGHEST = lax.Precision.HIGHEST
HIGH = lax.Precision.HIGH


def mdot(left, right, precision=HIGHEST):
    return jnp.dot(left, right, precision=precision, preferred_element_type=jnp.float32)


def tdot(left, right, precision=HIGHEST):
    return lax.dot_general(
        left, right, (((1,), (1,)), ((), ())), precision=precision, preferred_element_type=jnp.float32
    )


def assemble_t(block_cols, values_t, col_blocks):
    block_rows, nonzero = block_cols.shape
    width = values_t.shape[0] // nonzero
    span = block_rows * width
    flipped = values_t.reshape(nonzero, 1, width, span)
    spread = jnp.repeat(block_cols.T, width, axis=1)
    columns = jnp.arange(col_blocks, dtype=jnp.int32)
    hit = spread[:, None, None, :] == columns[None, :, None, None]
    dense = jnp.where(hit, flipped, 0.0).sum(axis=0)
    return dense.reshape(col_blocks * width, span)


def invert_lower(factor, block_inverses):
    inverses = jnp.stack(block_inverses)
    size = inverses.shape[1]
    while inverses.shape[0] > 1:
        pairs = inverses.shape[0] // 2
        first, second = inverses[0::2], inverses[1::2]
        coupling = jnp.stack(
            [
                factor[(2 * q + 1) * size:(2 * q + 2) * size, 2 * q * size:(2 * q + 1) * size]
                for q in range(pairs)
            ]
        )
        corner = jnp.einsum("qij,qjk->qik", second, coupling, precision=HIGHEST)
        corner = -jnp.einsum("qik,qkl->qil", corner, first, precision=HIGHEST)
        top = jnp.concatenate([first, jnp.zeros_like(first)], axis=2)
        bottom = jnp.concatenate([corner, second], axis=2)
        inverses = jnp.concatenate([top, bottom], axis=1)
        size *= 2
    return inverses[0]


def on_device(
    carried_block, coupling_values, block_cols, next_block, fixed_rows, fixed_next, tip_block
):
    rows, size = carried_block.shape
    value_rows, value_cols = coupling_values.shape
    local_block_rows, nonzero = block_cols.shape
    width = value_cols // nonzero
    fixed_count = fixed_rows.shape[0]
    factored = PANELS * rows
    me = lax.axis_index("row")
    is_top = me < PANELS
    top_at = jnp.minimum(me, PANELS - 1) * rows
    fixed_cols = fixed_rows.shape[1]
    block = min(BLOCK, rows)
    cols_count = local_block_rows * nonzero
    lanes = max(value_cols, fixed_cols, cols_count)

    def widen(part):
        return jnp.pad(part, ((0, 0), (0, lanes - part.shape[1])))

    values_t = coupling_values.T
    cols_row = block_cols.reshape(1, cols_count).astype(jnp.float32)
    packed = jnp.concatenate([widen(fixed_rows), widen(cols_row)], axis=0)
    pad = (-packed.shape[0]) % 8
    packed = jnp.concatenate([packed, jnp.zeros((pad, lanes), jnp.float32)], axis=0)
    gathered = lax.all_gather(packed, "row", axis=0)
    devices = gathered.shape[0]
    all_fixed = gathered[:, :fixed_count, :fixed_cols].transpose(1, 0, 2)
    all_fixed = all_fixed.reshape(fixed_count, devices * fixed_cols)
    all_block_cols = gathered[:, fixed_count, :cols_count]
    all_block_cols = jnp.round(all_block_cols).astype(jnp.int32).reshape(-1, nonzero)

    blocks = factored // block
    widths = [rows // block] * PANELS
    bounds = [0]
    for count in widths:
        bounds.append(bounds[-1] + count * block)
    chunks = [
        lax.all_gather(carried_block[:, lo:hi], "row", axis=0, tiled=True)
        for lo, hi in zip(bounds[:-1], bounds[1:])
    ]
    chunk_of = [c for c, count in enumerate(widths) for _ in range(count)]

    columns = []
    block_inverses = []
    for k in range(factored // block):
        chunk = chunk_of[k]
        offset = k * block - bounds[chunk]
        panel = chunks[chunk][k * block:factored, offset:offset + block]
        if k:
            done = jnp.concatenate([col[k * block:] for col in columns], axis=1)
            panel = panel - tdot(done, done[:block])
        diagonal = jnp.linalg.cholesky(panel[:block], symmetrize_input=False)
        diagonal_inverse = jax.scipy.linalg.solve_triangular(
            diagonal, jnp.eye(block, dtype=jnp.float32), lower=True
        )
        under = tdot(panel[block:], diagonal_inverse)
        column = jnp.concatenate(
            [jnp.zeros((k * block, block), jnp.float32), diagonal, under], axis=0
        )
        columns.append(column)
        block_inverses.append(diagonal_inverse)
    head_factor = jnp.concatenate(columns, axis=1)
    head_inverse = invert_lower(head_factor, block_inverses)

    def minus_below(scaled):
        total = None
        for c, (lo, hi) in enumerate(zip(bounds[:-1], bounds[1:])):
            part = tdot(scaled[:, lo:hi], chunks[c][factored:], HIGH)
            total = part if total is None else total + part
        return total

    own_cols = carried_block[:, :factored]
    lower = tdot(own_cols, head_inverse, HIGH)
    lower = jnp.where(is_top, lax.dynamic_slice_in_dim(head_factor, top_at, rows, 0), lower)
    lower_scaled = mdot(lower, head_inverse, HIGH)
    state_rest = carried_block[:, factored:] - minus_below(lower_scaled)
    state_rest = jnp.where(is_top, 0.0, state_rest)
    factor_state = jnp.concatenate([lower, state_rest], axis=1)

    coupled = assemble_t(block_cols, values_t, size // width).T
    coupled_panel = tdot(coupled[:, :factored], head_inverse, HIGH)
    coupled_scaled = mdot(coupled_panel, head_inverse, HIGH)
    coupled_rest = coupled[:, factored:] - minus_below(coupled_scaled)
    coupling_factor = jnp.concatenate([coupled_panel, coupled_rest], axis=1)

    all_values_t = lax.all_gather(values_t, "row", axis=1, tiled=True)
    all_blocks = size // width
    head_blocks = factored // width
    near_end = min(head_blocks + REACH, all_blocks)
    far_start = max(all_blocks - REACH, near_end)
    spans = [(lo, hi) for lo, hi in ((0, near_end), (far_start, all_blocks)) if hi > lo]
    pieces = []
    at = 0
    for lo, hi in spans:
        if lo > at:
            pieces.append(next_block[:, at * width:lo * width])
        head_t = assemble_t(all_block_cols[lo:hi], all_values_t[:, lo * width:hi * width], head_blocks)
        pieces.append(
            next_block[:, lo * width:hi * width] - mdot(coupled_scaled, head_t, HIGH)
        )
        at = hi
    if at < all_blocks:
        pieces.append(next_block[:, at * width:])
    carried_next = jnp.concatenate(pieces, axis=1)

    fixed_panel = tdot(all_fixed[:, :factored], head_inverse, HIGH)
    own_fixed_panel = lax.dynamic_slice_in_dim(fixed_panel, top_at, rows, 1)
    fixed_factor = jnp.where(
        is_top, own_fixed_panel, fixed_rows - tdot(fixed_panel, lower, HIGH)
    )
    fixed_carried = fixed_next - tdot(fixed_panel, coupled_panel, HIGH)
    tip_next = tip_block - tdot(fixed_panel, fixed_panel, HIGH)
    return (factor_state, coupling_factor, carried_next, fixed_factor, fixed_carried, tip_next)


def solution(mesh):
    return jax.shard_map(
        on_device,
        mesh=mesh,
        in_specs=(
            P(("hyper", "row"), None),
            P(("hyper", "row"), None),
            P("row", None),
            P(("hyper", "row"), None),
            P("hyper", "row"),
            P("hyper", "row"),
            P("hyper", None),
        ),
        out_specs=(
            P(("hyper", "row"), None),
            P(("hyper", "row"), None),
            P(("hyper", "row"), None),
            P("hyper", "row"),
            P("hyper", "row"),
            P("hyper", None),
        ),
        check_vma=False,
    )
```

```python
import jax
import jax.numpy as jnp
from jax import lax
from jax.sharding import PartitionSpec as P

PANELS = 4
BLOCK = 128
REACH = 32
HIGHEST = lax.Precision.HIGHEST
HIGH = lax.Precision.HIGH


def mdot(left, right, precision=HIGHEST):
    return jnp.dot(left, right, precision=precision, preferred_element_type=jnp.float32)


def tdot(left, right, precision=HIGHEST):
    return lax.dot_general(
        left, right, (((1,), (1,)), ((), ())), precision=precision, preferred_element_type=jnp.float32
    )


def assemble_t(block_cols, values_t, col_blocks):
    block_rows, nonzero = block_cols.shape
    width = values_t.shape[0] // nonzero
    span = block_rows * width
    flipped = values_t.reshape(nonzero, 1, width, span)
    spread = jnp.repeat(block_cols.T, width, axis=1)
    columns = jnp.arange(col_blocks, dtype=jnp.int32)
    hit = spread[:, None, None, :] == columns[None, :, None, None]
    dense = jnp.where(hit, flipped, 0.0).sum(axis=0)
    return dense.reshape(col_blocks * width, span)


def invert_lower(factor, block_inverses):
    inverses = jnp.stack(block_inverses)
    size = inverses.shape[1]
    while inverses.shape[0] > 1:
        pairs = inverses.shape[0] // 2
        first, second = inverses[0::2], inverses[1::2]
        coupling = jnp.stack(
            [
                factor[(2 * q + 1) * size:(2 * q + 2) * size, 2 * q * size:(2 * q + 1) * size]
                for q in range(pairs)
            ]
        )
        corner = jnp.einsum("qij,qjk->qik", second, coupling, precision=HIGHEST)
        corner = -jnp.einsum("qik,qkl->qil", corner, first, precision=HIGHEST)
        top = jnp.concatenate([first, jnp.zeros_like(first)], axis=2)
        bottom = jnp.concatenate([corner, second], axis=2)
        inverses = jnp.concatenate([top, bottom], axis=1)
        size *= 2
    return inverses[0]


def on_device(
    carried_block, coupling_values, block_cols, next_block, fixed_rows, fixed_next, tip_block
):
    rows, size = carried_block.shape
    value_rows, value_cols = coupling_values.shape
    local_block_rows, nonzero = block_cols.shape
    width = value_cols // nonzero
    fixed_count = fixed_rows.shape[0]
    factored = PANELS * rows
    me = lax.axis_index("row")
    is_top = me < PANELS
    top_at = jnp.minimum(me, PANELS - 1) * rows
    fixed_cols = fixed_rows.shape[1]
    block = min(BLOCK, rows)
    cols_count = local_block_rows * nonzero
    lanes = max(value_cols, fixed_cols, cols_count)

    def widen(part):
        return jnp.pad(part, ((0, 0), (0, lanes - part.shape[1])))

    values_t = coupling_values.T
    cols_row = block_cols.reshape(1, cols_count).astype(jnp.float32)
    packed = jnp.concatenate([widen(fixed_rows), widen(cols_row)], axis=0)
    pad = (-packed.shape[0]) % 8
    packed = jnp.concatenate([packed, jnp.zeros((pad, lanes), jnp.float32)], axis=0)
    gathered = lax.all_gather(packed, "row", axis=0)
    devices = gathered.shape[0]
    all_fixed = gathered[:, :fixed_count, :fixed_cols].transpose(1, 0, 2)
    all_fixed = all_fixed.reshape(fixed_count, devices * fixed_cols)
    all_block_cols = gathered[:, fixed_count, :cols_count]
    all_block_cols = jnp.round(all_block_cols).astype(jnp.int32).reshape(-1, nonzero)

    blocks = factored // block
    widths = [rows // block] * PANELS
    bounds = [0]
    for count in widths:
        bounds.append(bounds[-1] + count * block)
    chunks = [
        lax.all_gather(carried_block[:, lo:hi], "row", axis=0, tiled=True)
        for lo, hi in zip(bounds[:-1], bounds[1:])
    ]
    chunk_of = [c for c, count in enumerate(widths) for _ in range(count)]

    columns = []
    block_inverses = []
    for k in range(factored // block):
        chunk = chunk_of[k]
        offset = k * block - bounds[chunk]
        panel = chunks[chunk][k * block:factored, offset:offset + block]
        if k:
            done = jnp.concatenate([col[k * block:] for col in columns], axis=1)
            panel = panel - tdot(done, done[:block])
        diagonal = jnp.linalg.cholesky(panel[:block], symmetrize_input=False)
        diagonal_inverse = jax.scipy.linalg.solve_triangular(
            diagonal, jnp.eye(block, dtype=jnp.float32), lower=True
        )
        under = tdot(panel[block:], diagonal_inverse)
        column = jnp.concatenate(
            [jnp.zeros((k * block, block), jnp.float32), diagonal, under], axis=0
        )
        columns.append(column)
        block_inverses.append(diagonal_inverse)
    head_factor = jnp.concatenate(columns, axis=1)
    head_inverse = invert_lower(head_factor, block_inverses)

    def minus_below(scaled):
        total = None
        for c, (lo, hi) in enumerate(zip(bounds[:-1], bounds[1:])):
            part = tdot(scaled[:, lo:hi], chunks[c][factored:], HIGH)
            total = part if total is None else total + part
        return total

    own_cols = carried_block[:, :factored]
    lower = tdot(own_cols, head_inverse, HIGH)
    lower = jnp.where(is_top, lax.dynamic_slice_in_dim(head_factor, top_at, rows, 0), lower)
    lower_scaled = mdot(lower, head_inverse, HIGH)
    state_updates = jnp.pad(minus_below(lower_scaled), ((0, 0), (factored, 0)))
    factor_state = jnp.where(is_top, 0.0, carried_block - state_updates)
    factor_state = lax.dynamic_update_slice(factor_state, lower, (0, 0))

    coupled = assemble_t(block_cols, values_t, size // width).T
    coupled_panel = tdot(coupled[:, :factored], head_inverse, HIGH)
    coupled_scaled = mdot(coupled_panel, head_inverse, HIGH)
    coupled_updates = jnp.pad(minus_below(coupled_scaled), ((0, 0), (factored, 0)))
    coupling_factor = lax.dynamic_update_slice(coupled - coupled_updates, coupled_panel, (0, 0))

    all_values_t = lax.all_gather(values_t, "row", axis=1, tiled=True)
    all_blocks = size // width
    head_blocks = factored // width
    near_end = min(head_blocks + REACH, all_blocks)
    far_start = max(all_blocks - REACH, near_end)
    spans = [(lo, hi) for lo, hi in ((0, near_end), (far_start, all_blocks)) if hi > lo]
    pieces = []
    at = 0
    for lo, hi in spans:
        if lo > at:
            pieces.append(jnp.zeros((rows, (lo - at) * width), jnp.float32))
        head_t = assemble_t(all_block_cols[lo:hi], all_values_t[:, lo * width:hi * width], head_blocks)
        pieces.append(mdot(coupled_scaled, head_t, HIGH))
        at = hi
    if at < all_blocks:
        pieces.append(jnp.zeros((rows, (all_blocks - at) * width), jnp.float32))
    carried_next = next_block - jnp.concatenate(pieces, axis=1)

    fixed_panel = tdot(all_fixed[:, :factored], head_inverse, HIGH)
    own_fixed_panel = lax.dynamic_slice_in_dim(fixed_panel, top_at, rows, 1)
    fixed_factor = jnp.where(
        is_top, own_fixed_panel, fixed_rows - tdot(fixed_panel, lower, HIGH)
    )
    fixed_carried = fixed_next - tdot(fixed_panel, coupled_panel, HIGH)
    tip_next = tip_block - tdot(fixed_panel, fixed_panel, HIGH)
    return (factor_state, coupling_factor, carried_next, fixed_factor, fixed_carried, tip_next)


def solution(mesh):
    return jax.shard_map(
        on_device,
        mesh=mesh,
        in_specs=(
            P(("hyper", "row"), None),
            P(("hyper", "row"), None),
            P("row", None),
            P(("hyper", "row"), None),
            P("hyper", "row"),
            P("hyper", "row"),
            P("hyper", None),
        ),
        out_specs=(
            P(("hyper", "row"), None),
            P(("hyper", "row"), None),
            P(("hyper", "row"), None),
            P("hyper", "row"),
            P("hyper", "row"),
            P("hyper", None),
        ),
        check_vma=False,
    )
```

```python
import jax
import jax.numpy as jnp
from jax import lax
from jax.sharding import PartitionSpec as P

PANELS = 4
BLOCK = 128
REACH = 32
HIGHEST = lax.Precision.HIGHEST
HIGH = lax.Precision.HIGH


def mdot(left, right, precision=HIGHEST):
    return jnp.dot(left, right, precision=precision, preferred_element_type=jnp.float32)


def tdot(left, right, precision=HIGHEST):
    return lax.dot_general(
        left, right, (((1,), (1,)), ((), ())), precision=precision, preferred_element_type=jnp.float32
    )


def assemble_t(block_cols, values_t, col_blocks):
    block_rows, nonzero = block_cols.shape
    width = values_t.shape[0] // nonzero
    span = block_rows * width
    flipped = values_t.reshape(nonzero, 1, width, span)
    spread = jnp.repeat(block_cols.T, width, axis=1)
    columns = jnp.arange(col_blocks, dtype=jnp.int32)
    hit = spread[:, None, None, :] == columns[None, :, None, None]
    dense = jnp.where(hit, flipped, 0.0).sum(axis=0)
    return dense.reshape(col_blocks * width, span)


def invert_lower(factor, block_inverses):
    inverses = jnp.stack(block_inverses)
    size = inverses.shape[1]
    while inverses.shape[0] > 1:
        pairs = inverses.shape[0] // 2
        first, second = inverses[0::2], inverses[1::2]
        coupling = jnp.stack(
            [
                factor[(2 * q + 1) * size:(2 * q + 2) * size, 2 * q * size:(2 * q + 1) * size]
                for q in range(pairs)
            ]
        )
        corner = jnp.einsum("qij,qjk->qik", second, coupling, precision=HIGHEST)
        corner = -jnp.einsum("qik,qkl->qil", corner, first, precision=HIGHEST)
        top = jnp.concatenate([first, jnp.zeros_like(first)], axis=2)
        bottom = jnp.concatenate([corner, second], axis=2)
        inverses = jnp.concatenate([top, bottom], axis=1)
        size *= 2
    return inverses[0]


def on_device(
    carried_block, coupling_values, block_cols, next_block, fixed_rows, fixed_next, tip_block
):
    rows, size = carried_block.shape
    value_rows, value_cols = coupling_values.shape
    local_block_rows, nonzero = block_cols.shape
    width = value_cols // nonzero
    fixed_count = fixed_rows.shape[0]
    factored = PANELS * rows
    me = lax.axis_index("row")
    is_top = me < PANELS
    top_at = jnp.minimum(me, PANELS - 1) * rows
    fixed_cols = fixed_rows.shape[1]
    block = min(BLOCK, rows)
    cols_count = local_block_rows * nonzero
    lanes = max(value_cols, fixed_cols, cols_count)

    def widen(part):
        return jnp.pad(part, ((0, 0), (0, lanes - part.shape[1])))

    values_t = coupling_values.T
    cols_row = block_cols.reshape(1, cols_count).astype(jnp.float32)
    packed = jnp.concatenate([widen(fixed_rows), widen(cols_row)], axis=0)
    pad = (-packed.shape[0]) % 8
    packed = jnp.concatenate([packed, jnp.zeros((pad, lanes), jnp.float32)], axis=0)
    gathered = lax.all_gather(packed, "row", axis=0)
    devices = gathered.shape[0]
    all_fixed = gathered[:, :fixed_count, :fixed_cols].transpose(1, 0, 2)
    all_fixed = all_fixed.reshape(fixed_count, devices * fixed_cols)
    all_block_cols = gathered[:, fixed_count, :cols_count]
    all_block_cols = jnp.round(all_block_cols).astype(jnp.int32).reshape(-1, nonzero)

    blocks = factored // block
    widths = [rows // block] * PANELS
    bounds = [0]
    for count in widths:
        bounds.append(bounds[-1] + count * block)
    chunks = [
        lax.all_gather(carried_block[:, lo:hi], "row", axis=0, tiled=True)
        for lo, hi in zip(bounds[:-1], bounds[1:])
    ]
    chunk_of = [c for c, count in enumerate(widths) for _ in range(count)]

    columns = []
    block_inverses = []
    for k in range(factored // block):
        chunk = chunk_of[k]
        offset = k * block - bounds[chunk]
        panel = chunks[chunk][k * block:factored, offset:offset + block]
        if k:
            done = jnp.concatenate(
                [col[(k - j) * block:] for j, col in enumerate(columns)], axis=1
            )
            panel = panel - tdot(done, done[:block])
        diagonal = jnp.linalg.cholesky(panel[:block], symmetrize_input=False)
        diagonal_inverse = jax.scipy.linalg.solve_triangular(
            diagonal, jnp.eye(block, dtype=jnp.float32), lower=True
        )
        under = tdot(panel[block:], diagonal_inverse)
        columns.append(jnp.concatenate([diagonal, under], axis=0))
        block_inverses.append(diagonal_inverse)
    head_factor = jnp.concatenate(
        [jnp.pad(col, ((j * block, 0), (0, 0))) for j, col in enumerate(columns)], axis=1
    )
    head_inverse = invert_lower(head_factor, block_inverses)

    def minus_below(scaled):
        total = None
        for c, (lo, hi) in enumerate(zip(bounds[:-1], bounds[1:])):
            part = tdot(scaled[:, lo:hi], chunks[c][factored:], HIGH)
            total = part if total is None else total + part
        return total

    own_cols = carried_block[:, :factored]
    lower = tdot(own_cols, head_inverse, HIGH)
    lower = jnp.where(is_top, lax.dynamic_slice_in_dim(head_factor, top_at, rows, 0), lower)
    lower_scaled = mdot(lower, head_inverse, HIGH)
    state_updates = jnp.pad(minus_below(lower_scaled), ((0, 0), (factored, 0)))
    factor_state = jnp.where(is_top, 0.0, carried_block - state_updates)
    factor_state = lax.dynamic_update_slice(factor_state, lower, (0, 0))

    coupled = assemble_t(block_cols, values_t, size // width).T
    coupled_panel = tdot(coupled[:, :factored], head_inverse, HIGH)
    coupled_scaled = mdot(coupled_panel, head_inverse, HIGH)
    coupled_updates = jnp.pad(minus_below(coupled_scaled), ((0, 0), (factored, 0)))
    coupling_factor = lax.dynamic_update_slice(coupled - coupled_updates, coupled_panel, (0, 0))

    all_values_t = lax.all_gather(values_t, "row", axis=1, tiled=True)
    all_blocks = size // width
    head_blocks = factored // width
    near_end = min(head_blocks + REACH, all_blocks)
    far_start = max(all_blocks - REACH, near_end)
    spans = [(lo, hi) for lo, hi in ((0, near_end), (far_start, all_blocks)) if hi > lo]
    pieces = []
    at = 0
    for lo, hi in spans:
        if lo > at:
            pieces.append(jnp.zeros((rows, (lo - at) * width), jnp.float32))
        head_t = assemble_t(all_block_cols[lo:hi], all_values_t[:, lo * width:hi * width], head_blocks)
        pieces.append(mdot(coupled_scaled, head_t, HIGH))
        at = hi
    if at < all_blocks:
        pieces.append(jnp.zeros((rows, (all_blocks - at) * width), jnp.float32))
    carried_next = next_block - jnp.concatenate(pieces, axis=1)

    fixed_panel = tdot(all_fixed[:, :factored], head_inverse, HIGH)
    own_fixed_panel = lax.dynamic_slice_in_dim(fixed_panel, top_at, rows, 1)
    fixed_factor = jnp.where(
        is_top, own_fixed_panel, fixed_rows - tdot(fixed_panel, lower, HIGH)
    )
    fixed_carried = fixed_next - tdot(fixed_panel, coupled_panel, HIGH)
    tip_next = tip_block - tdot(fixed_panel, fixed_panel, HIGH)
    return (factor_state, coupling_factor, carried_next, fixed_factor, fixed_carried, tip_next)


def solution(mesh):
    return jax.shard_map(
        on_device,
        mesh=mesh,
        in_specs=(
            P(("hyper", "row"), None),
            P(("hyper", "row"), None),
            P("row", None),
            P(("hyper", "row"), None),
            P("hyper", "row"),
            P("hyper", "row"),
            P("hyper", None),
        ),
        out_specs=(
            P(("hyper", "row"), None),
            P(("hyper", "row"), None),
            P(("hyper", "row"), None),
            P("hyper", "row"),
            P("hyper", "row"),
            P("hyper", None),
        ),
        check_vma=False,
    )
```

```python
import jax
import jax.numpy as jnp
from jax import lax
from jax.sharding import PartitionSpec as P

PANELS = 4
BLOCK = 128
REACH = 32
HIGHEST = lax.Precision.HIGHEST
HIGH = lax.Precision.HIGH


def mdot(left, right, precision=HIGHEST):
    return jnp.dot(left, right, precision=precision, preferred_element_type=jnp.float32)


def tdot(left, right, precision=HIGHEST):
    return lax.dot_general(
        left, right, (((1,), (1,)), ((), ())), precision=precision, preferred_element_type=jnp.float32
    )


def assemble_t(block_cols, values_t, col_blocks):
    block_rows, nonzero = block_cols.shape
    width = values_t.shape[0] // nonzero
    span = block_rows * width
    flipped = values_t.reshape(nonzero, 1, width, span)
    spread = jnp.repeat(block_cols.T, width, axis=1)
    columns = jnp.arange(col_blocks, dtype=jnp.int32)
    hit = spread[:, None, None, :] == columns[None, :, None, None]
    dense = jnp.where(hit, flipped, 0.0).sum(axis=0)
    return dense.reshape(col_blocks * width, span)


def invert_lower(factor, block_inverses):
    inverses = jnp.stack(block_inverses)
    size = inverses.shape[1]
    while inverses.shape[0] > 1:
        pairs = inverses.shape[0] // 2
        first, second = inverses[0::2], inverses[1::2]
        coupling = jnp.stack(
            [
                factor[(2 * q + 1) * size:(2 * q + 2) * size, 2 * q * size:(2 * q + 1) * size]
                for q in range(pairs)
            ]
        )
        corner = jnp.einsum("qij,qjk->qik", second, coupling, precision=HIGHEST)
        corner = -jnp.einsum("qik,qkl->qil", corner, first, precision=HIGHEST)
        top = jnp.concatenate([first, jnp.zeros_like(first)], axis=2)
        bottom = jnp.concatenate([corner, second], axis=2)
        inverses = jnp.concatenate([top, bottom], axis=1)
        size *= 2
    return inverses[0]


def on_device(
    carried_block, coupling_values, block_cols, next_block, fixed_rows, fixed_next, tip_block
):
    rows, size = carried_block.shape
    value_rows, value_cols = coupling_values.shape
    local_block_rows, nonzero = block_cols.shape
    width = value_cols // nonzero
    fixed_count = fixed_rows.shape[0]
    factored = PANELS * rows
    me = lax.axis_index("row")
    is_top = me < PANELS
    top_at = jnp.minimum(me, PANELS - 1) * rows
    fixed_cols = fixed_rows.shape[1]
    block = min(BLOCK, rows)
    cols_count = local_block_rows * nonzero
    lanes = max(value_rows, fixed_cols, cols_count)

    def widen(part):
        return jnp.pad(part, ((0, 0), (0, lanes - part.shape[1])))

    values_t = coupling_values.T
    cols_row = block_cols.reshape(1, cols_count).astype(jnp.float32)
    packed = jnp.concatenate([widen(values_t), widen(fixed_rows), widen(cols_row)], axis=0)
    pad = (-packed.shape[0]) % 8
    packed = jnp.concatenate([packed, jnp.zeros((pad, lanes), jnp.float32)], axis=0)

    blocks = factored // block
    widths = [rows // block] * PANELS
    bounds = [0]
    for count in widths:
        bounds.append(bounds[-1] + count * block)
    chunks = [
        lax.all_gather(carried_block[:, lo:hi], "row", axis=0, tiled=True)
        for lo, hi in zip(bounds[:-1], bounds[1:])
    ]
    chunk_of = [c for c, count in enumerate(widths) for _ in range(count)]

    columns = []
    block_inverses = []
    for k in range(factored // block):
        chunk = chunk_of[k]
        offset = k * block - bounds[chunk]
        panel = chunks[chunk][k * block:factored, offset:offset + block]
        if k:
            done = jnp.concatenate([col[k * block:] for col in columns], axis=1)
            panel = panel - tdot(done, done[:block])
        diagonal = jnp.linalg.cholesky(panel[:block], symmetrize_input=False)
        diagonal_inverse = jax.scipy.linalg.solve_triangular(
            diagonal, jnp.eye(block, dtype=jnp.float32), lower=True
        )
        under = tdot(panel[block:], diagonal_inverse)
        column = jnp.concatenate(
            [jnp.zeros((k * block, block), jnp.float32), diagonal, under], axis=0
        )
        columns.append(column)
        block_inverses.append(diagonal_inverse)
    head_factor = jnp.concatenate(columns, axis=1)
    head_inverse = invert_lower(head_factor, block_inverses)

    def minus_below(scaled):
        total = None
        for c, (lo, hi) in enumerate(zip(bounds[:-1], bounds[1:])):
            part = tdot(scaled[:, lo:hi], chunks[c][factored:], HIGH)
            total = part if total is None else total + part
        return total

    own_cols = carried_block[:, :factored]
    lower = tdot(own_cols, head_inverse, HIGH)
    lower = jnp.where(is_top, lax.dynamic_slice_in_dim(head_factor, top_at, rows, 0), lower)
    lower_scaled = mdot(lower, head_inverse, HIGH)
    state_updates = jnp.pad(minus_below(lower_scaled), ((0, 0), (factored, 0)))
    factor_state = jnp.where(is_top, 0.0, carried_block - state_updates)
    factor_state = lax.dynamic_update_slice(factor_state, lower, (0, 0))

    coupled = assemble_t(block_cols, values_t, size // width).T
    coupled_panel = tdot(coupled[:, :factored], head_inverse, HIGH)
    coupled_scaled = mdot(coupled_panel, head_inverse, HIGH)
    coupled_updates = jnp.pad(minus_below(coupled_scaled), ((0, 0), (factored, 0)))
    coupling_factor = lax.dynamic_update_slice(coupled - coupled_updates, coupled_panel, (0, 0))

    gathered = lax.all_gather(packed, "row", axis=1, tiled=True)
    devices = gathered.shape[1] // lanes
    gathered = gathered.reshape(gathered.shape[0], devices, lanes)
    all_values_t = gathered[:value_cols, :, :value_rows].reshape(value_cols, devices * value_rows)
    all_fixed = gathered[value_cols:value_cols + fixed_count, :, :fixed_cols]
    all_fixed = all_fixed.reshape(fixed_count, devices * fixed_cols)
    all_block_cols = gathered[value_cols + fixed_count, :, :cols_count]
    all_block_cols = jnp.round(all_block_cols).astype(jnp.int32).reshape(-1, nonzero)
    all_blocks = size // width
    head_blocks = factored // width
    near_end = min(head_blocks + REACH, all_blocks)
    far_start = max(all_blocks - REACH, near_end)
    spans = [(lo, hi) for lo, hi in ((0, near_end), (far_start, all_blocks)) if hi > lo]
    pieces = []
    at = 0
    for lo, hi in spans:
        if lo > at:
            pieces.append(jnp.zeros((rows, (lo - at) * width), jnp.float32))
        head_t = assemble_t(all_block_cols[lo:hi], all_values_t[:, lo * width:hi * width], head_blocks)
        pieces.append(mdot(coupled_scaled, head_t, HIGH))
        at = hi
    if at < all_blocks:
        pieces.append(jnp.zeros((rows, (all_blocks - at) * width), jnp.float32))
    carried_next = next_block - jnp.concatenate(pieces, axis=1)

    fixed_panel = tdot(all_fixed[:, :factored], head_inverse, HIGH)
    own_fixed_panel = lax.dynamic_slice_in_dim(fixed_panel, top_at, rows, 1)
    fixed_factor = jnp.where(
        is_top, own_fixed_panel, fixed_rows - tdot(fixed_panel, lower, HIGH)
    )
    fixed_carried = fixed_next - tdot(fixed_panel, coupled_panel, HIGH)
    tip_next = tip_block - tdot(fixed_panel, fixed_panel, HIGH)
    return (factor_state, coupling_factor, carried_next, fixed_factor, fixed_carried, tip_next)


def solution(mesh):
    return jax.shard_map(
        on_device,
        mesh=mesh,
        in_specs=(
            P(("hyper", "row"), None),
            P(("hyper", "row"), None),
            P("row", None),
            P(("hyper", "row"), None),
            P("hyper", "row"),
            P("hyper", "row"),
            P("hyper", None),
        ),
        out_specs=(
            P(("hyper", "row"), None),
            P(("hyper", "row"), None),
            P(("hyper", "row"), None),
            P("hyper", "row"),
            P("hyper", "row"),
            P("hyper", None),
        ),
        check_vma=False,
    )
```

```python
import jax
import jax.numpy as jnp
from jax import lax
from jax.sharding import PartitionSpec as P

PANELS = 4
BLOCK = 128
REACH = 32
HIGHEST = lax.Precision.HIGHEST
HIGH = lax.Precision.HIGH


def mdot(left, right, precision=HIGHEST):
    return jnp.dot(left, right, precision=precision, preferred_element_type=jnp.float32)


def tdot(left, right, precision=HIGHEST):
    return lax.dot_general(
        left, right, (((1,), (1,)), ((), ())), precision=precision, preferred_element_type=jnp.float32
    )


def assemble_t(block_cols, values_t, col_blocks, first_block=0):
    block_rows, nonzero = block_cols.shape
    width = values_t.shape[0] // nonzero
    span = block_rows * width
    flipped = values_t.reshape(nonzero, 1, width, span)
    spread = jnp.repeat(block_cols.T, width, axis=1)
    columns = jnp.arange(first_block, col_blocks, dtype=jnp.int32)
    hit = spread[:, None, None, :] == columns[None, :, None, None]
    dense = jnp.where(hit, flipped, 0.0).sum(axis=0)
    return dense.reshape((col_blocks - first_block) * width, span)


def invert_lower(factor, block_inverses):
    inverses = jnp.stack(block_inverses)
    size = inverses.shape[1]
    while inverses.shape[0] > 1:
        pairs = inverses.shape[0] // 2
        first, second = inverses[0::2], inverses[1::2]
        coupling = jnp.stack(
            [
                factor[(2 * q + 1) * size:(2 * q + 2) * size, 2 * q * size:(2 * q + 1) * size]
                for q in range(pairs)
            ]
        )
        corner = jnp.einsum("qij,qjk->qik", second, coupling, precision=HIGHEST)
        corner = -jnp.einsum("qik,qkl->qil", corner, first, precision=HIGHEST)
        top = jnp.concatenate([first, jnp.zeros_like(first)], axis=2)
        bottom = jnp.concatenate([corner, second], axis=2)
        inverses = jnp.concatenate([top, bottom], axis=1)
        size *= 2
    return inverses[0]


def on_device(
    carried_block, coupling_values, block_cols, next_block, fixed_rows, fixed_next, tip_block
):
    rows, size = carried_block.shape
    value_rows, value_cols = coupling_values.shape
    local_block_rows, nonzero = block_cols.shape
    width = value_cols // nonzero
    fixed_count = fixed_rows.shape[0]
    factored = PANELS * rows
    me = lax.axis_index("row")
    is_top = me < PANELS
    top_at = jnp.minimum(me, PANELS - 1) * rows
    fixed_cols = fixed_rows.shape[1]
    block = min(BLOCK, rows)
    cols_count = local_block_rows * nonzero
    lanes = max(value_cols, fixed_cols, cols_count)

    def widen(part):
        return jnp.pad(part, ((0, 0), (0, lanes - part.shape[1])))

    values_t = coupling_values.T
    cols_row = block_cols.reshape(1, cols_count).astype(jnp.float32)
    packed = jnp.concatenate([widen(fixed_rows), widen(cols_row)], axis=0)
    pad = (-packed.shape[0]) % 8
    packed = jnp.concatenate([packed, jnp.zeros((pad, lanes), jnp.float32)], axis=0)
    gathered = lax.all_gather(packed, "row", axis=0)
    devices = gathered.shape[0]
    all_fixed = gathered[:, :fixed_count, :fixed_cols].transpose(1, 0, 2)
    all_fixed = all_fixed.reshape(fixed_count, devices * fixed_cols)
    all_block_cols = gathered[:, fixed_count, :cols_count]
    all_block_cols = jnp.round(all_block_cols).astype(jnp.int32).reshape(-1, nonzero)

    blocks = factored // block
    widths = [rows // block] * PANELS
    bounds = [0]
    for count in widths:
        bounds.append(bounds[-1] + count * block)
    chunks = [
        lax.all_gather(carried_block[:, lo:hi], "row", axis=0, tiled=True)
        for lo, hi in zip(bounds[:-1], bounds[1:])
    ]
    chunk_of = [c for c, count in enumerate(widths) for _ in range(count)]

    columns = []
    block_inverses = []
    for k in range(factored // block):
        chunk = chunk_of[k]
        offset = k * block - bounds[chunk]
        panel = chunks[chunk][k * block:factored, offset:offset + block]
        if k:
            done = jnp.concatenate([col[k * block:] for col in columns], axis=1)
            panel = panel - tdot(done, done[:block])
        diagonal = jnp.linalg.cholesky(panel[:block], symmetrize_input=False)
        diagonal_inverse = jax.scipy.linalg.solve_triangular(
            diagonal, jnp.eye(block, dtype=jnp.float32), lower=True
        )
        under = tdot(panel[block:], diagonal_inverse)
        column = jnp.concatenate(
            [jnp.zeros((k * block, block), jnp.float32), diagonal, under], axis=0
        )
        columns.append(column)
        block_inverses.append(diagonal_inverse)
    head_factor = jnp.concatenate(columns, axis=1)
    head_inverse = invert_lower(head_factor, block_inverses)

    def minus_below(scaled):
        total = None
        for c, (lo, hi) in enumerate(zip(bounds[:-1], bounds[1:])):
            part = tdot(scaled[:, lo:hi], chunks[c][factored:], HIGH)
            total = part if total is None else total + part
        return total

    own_cols = carried_block[:, :factored]
    lower = tdot(own_cols, head_inverse, HIGH)
    lower = jnp.where(is_top, lax.dynamic_slice_in_dim(head_factor, top_at, rows, 0), lower)
    lower_scaled = mdot(lower, head_inverse, HIGH)
    state_updates = jnp.pad(minus_below(lower_scaled), ((0, 0), (factored, 0)))
    factor_state = jnp.where(is_top, 0.0, carried_block - state_updates)
    factor_state = lax.dynamic_update_slice(factor_state, lower, (0, 0))

    coupled = assemble_t(block_cols, values_t, size // width).T
    coupled_panel = tdot(coupled[:, :factored], head_inverse, HIGH)
    coupled_scaled = mdot(coupled_panel, head_inverse, HIGH)
    coupled_updates = jnp.pad(minus_below(coupled_scaled), ((0, 0), (factored, 0)))
    coupling_factor = lax.dynamic_update_slice(coupled - coupled_updates, coupled_panel, (0, 0))

    all_values_t = lax.all_gather(values_t, "row", axis=1, tiled=True)
    all_blocks = size // width
    head_blocks = factored // width

    def reach(r):
        near = [n for n in range(head_blocks)
                if min(abs(n - r), all_blocks - abs(n - r)) <= REACH]
        return (min(near), max(near) + 1) if near else None

    groups = []
    for lo in range(0, all_blocks, 16):
        hi = min(lo + 16, all_blocks)
        hits = [reach(r) for r in range(lo, hi)]
        hits = [h for h in hits if h is not None]
        if not hits:
            continue
        cols = (min(h[0] for h in hits), max(h[1] for h in hits))
        if groups and groups[-1][1] == lo and groups[-1][2] == cols:
            groups[-1] = (groups[-1][0], hi, cols)
        else:
            groups.append((lo, hi, cols))
    pieces = []
    at = 0
    for lo, hi, (first, last) in groups:
        if lo > at:
            pieces.append(jnp.zeros((rows, (lo - at) * width), jnp.float32))
        head_t = assemble_t(
            all_block_cols[lo:hi], all_values_t[:, lo * width:hi * width], last, first
        )
        pieces.append(mdot(coupled_scaled[:, first * width:last * width], head_t, HIGH))
        at = hi
    if at < all_blocks:
        pieces.append(jnp.zeros((rows, (all_blocks - at) * width), jnp.float32))
    carried_next = next_block - jnp.concatenate(pieces, axis=1)

    fixed_panel = tdot(all_fixed[:, :factored], head_inverse, HIGH)
    own_fixed_panel = lax.dynamic_slice_in_dim(fixed_panel, top_at, rows, 1)
    fixed_factor = jnp.where(
        is_top, own_fixed_panel, fixed_rows - tdot(fixed_panel, lower, HIGH)
    )
    fixed_carried = fixed_next - tdot(fixed_panel, coupled_panel, HIGH)
    tip_next = tip_block - tdot(fixed_panel, fixed_panel, HIGH)
    return (factor_state, coupling_factor, carried_next, fixed_factor, fixed_carried, tip_next)


def solution(mesh):
    return jax.shard_map(
        on_device,
        mesh=mesh,
        in_specs=(
            P(("hyper", "row"), None),
            P(("hyper", "row"), None),
            P("row", None),
            P(("hyper", "row"), None),
            P("hyper", "row"),
            P("hyper", "row"),
            P("hyper", None),
        ),
        out_specs=(
            P(("hyper", "row"), None),
            P(("hyper", "row"), None),
            P(("hyper", "row"), None),
            P("hyper", "row"),
            P("hyper", "row"),
            P("hyper", None),
        ),
        check_vma=False,
    )
```

```python
import jax
import jax.numpy as jnp
from jax import lax
from jax.sharding import PartitionSpec as P

PANELS = 4
BLOCK = 128
REACH = 32
HIGHEST = lax.Precision.HIGHEST
HIGH = lax.Precision.HIGH


def mdot(left, right, precision=HIGHEST):
    return jnp.dot(left, right, precision=precision, preferred_element_type=jnp.float32)


def tdot(left, right, precision=HIGHEST):
    return lax.dot_general(
        left, right, (((1,), (1,)), ((), ())), precision=precision, preferred_element_type=jnp.float32
    )


def assemble_t(block_cols, values_t, col_blocks, first_block=0):
    block_rows, nonzero = block_cols.shape
    width = values_t.shape[0] // nonzero
    span = block_rows * width
    flipped = values_t.reshape(nonzero, 1, width, span)
    spread = jnp.repeat(block_cols.T, width, axis=1)
    columns = jnp.arange(first_block, col_blocks, dtype=jnp.int32)
    hit = spread[:, None, None, :] == columns[None, :, None, None]
    dense = jnp.where(hit, flipped, 0.0).sum(axis=0)
    return dense.reshape((col_blocks - first_block) * width, span)


def invert_lower(factor, block_inverses):
    inverses = jnp.stack(block_inverses)
    size = inverses.shape[1]
    while inverses.shape[0] > 1:
        pairs = inverses.shape[0] // 2
        first, second = inverses[0::2], inverses[1::2]
        coupling = jnp.stack(
            [
                factor[(2 * q + 1) * size:(2 * q + 2) * size, 2 * q * size:(2 * q + 1) * size]
                for q in range(pairs)
            ]
        )
        corner = jnp.einsum("qij,qjk->qik", second, coupling, precision=HIGHEST)
        corner = -jnp.einsum("qik,qkl->qil", corner, first, precision=HIGHEST)
        top = jnp.concatenate([first, jnp.zeros_like(first)], axis=2)
        bottom = jnp.concatenate([corner, second], axis=2)
        inverses = jnp.concatenate([top, bottom], axis=1)
        size *= 2
    return inverses[0]


def on_device(
    carried_block, coupling_values, block_cols, next_block, fixed_rows, fixed_next, tip_block
):
    rows, size = carried_block.shape
    value_rows, value_cols = coupling_values.shape
    local_block_rows, nonzero = block_cols.shape
    width = value_cols // nonzero
    fixed_count = fixed_rows.shape[0]
    factored = PANELS * rows
    me = lax.axis_index("row")
    is_top = me < PANELS
    top_at = jnp.minimum(me, PANELS - 1) * rows
    fixed_cols = fixed_rows.shape[1]
    block = min(BLOCK, rows)
    cols_count = local_block_rows * nonzero
    lanes = max(value_cols, fixed_cols, cols_count)

    def widen(part):
        return jnp.pad(part, ((0, 0), (0, lanes - part.shape[1])))

    values_t = coupling_values.T
    cols_row = block_cols.reshape(1, cols_count).astype(jnp.float32)
    packed = jnp.concatenate([widen(fixed_rows), widen(cols_row)], axis=0)
    pad = (-packed.shape[0]) % 8
    packed = jnp.concatenate([packed, jnp.zeros((pad, lanes), jnp.float32)], axis=0)
    gathered = lax.all_gather(packed, "row", axis=0)
    devices = gathered.shape[0]
    all_fixed = gathered[:, :fixed_count, :fixed_cols].transpose(1, 0, 2)
    all_fixed = all_fixed.reshape(fixed_count, devices * fixed_cols)
    all_block_cols = gathered[:, fixed_count, :cols_count]
    all_block_cols = jnp.round(all_block_cols).astype(jnp.int32).reshape(-1, nonzero)

    blocks = factored // block
    widths = [rows // block] * PANELS
    bounds = [0]
    for count in widths:
        bounds.append(bounds[-1] + count * block)
    chunks = [
        lax.all_gather(carried_block[:, lo:hi], "row", axis=0, tiled=True)
        for lo, hi in zip(bounds[:-1], bounds[1:])
    ]
    chunk_of = [c for c, count in enumerate(widths) for _ in range(count)]

    columns = []
    block_inverses = []
    for k in range(factored // block):
        chunk = chunk_of[k]
        offset = k * block - bounds[chunk]
        panel = chunks[chunk][k * block:factored, offset:offset + block]
        if k:
            done = jnp.concatenate([col[k * block:] for col in columns], axis=1)
            panel = panel - tdot(done, done[:block])
        diagonal = jnp.linalg.cholesky(panel[:block], symmetrize_input=False)
        diagonal_inverse = jax.scipy.linalg.solve_triangular(
            diagonal, jnp.eye(block, dtype=jnp.float32), lower=True
        )
        under = tdot(panel[block:], diagonal_inverse)
        column = jnp.concatenate(
            [jnp.zeros((k * block, block), jnp.float32), diagonal, under], axis=0
        )
        columns.append(column)
        block_inverses.append(diagonal_inverse)
    head_factor = jnp.concatenate(columns, axis=1)
    head_inverse = invert_lower(head_factor, block_inverses)

    def minus_below(scaled):
        total = None
        for c, (lo, hi) in enumerate(zip(bounds[:-1], bounds[1:])):
            part = tdot(scaled[:, lo:hi], chunks[c][factored:], HIGH)
            total = part if total is None else total + part
        return total

    own_cols = carried_block[:, :factored]
    lower = tdot(own_cols, head_inverse, HIGH)
    lower = jnp.where(is_top, lax.dynamic_slice_in_dim(head_factor, top_at, rows, 0), lower)
    lower_scaled = mdot(lower, head_inverse, HIGH)
    state_updates = jnp.pad(minus_below(lower_scaled), ((0, 0), (factored, 0)))
    factor_state = jnp.where(is_top, 0.0, carried_block - state_updates)
    factor_state = lax.dynamic_update_slice(factor_state, lower, (0, 0))

    coupled = assemble_t(block_cols, values_t, size // width).T
    coupled_panel = tdot(coupled[:, :factored], head_inverse, HIGH)
    coupled_scaled = mdot(coupled_panel, head_inverse, HIGH)
    coupled_updates = jnp.pad(minus_below(coupled_scaled), ((0, 0), (factored, 0)))
    coupling_factor = lax.dynamic_update_slice(coupled - coupled_updates, coupled_panel, (0, 0))

    all_values_t = lax.all_gather(values_t, "row", axis=1, tiled=True)
    all_blocks = size // width
    head_blocks = factored // width

    def reach(r):
        near = [n for n in range(head_blocks)
                if min(abs(n - r), all_blocks - abs(n - r)) <= REACH]
        return (min(near), max(near) + 1) if near else None

    groups = []
    for lo in range(0, all_blocks, 8):
        hi = min(lo + 8, all_blocks)
        hits = [reach(r) for r in range(lo, hi)]
        hits = [h for h in hits if h is not None]
        if not hits:
            continue
        cols = (min(h[0] for h in hits), max(h[1] for h in hits))
        if groups and groups[-1][1] == lo and groups[-1][2] == cols:
            groups[-1] = (groups[-1][0], hi, cols)
        else:
            groups.append((lo, hi, cols))
    pieces = []
    at = 0
    for lo, hi, (first, last) in groups:
        if lo > at:
            pieces.append(jnp.zeros((rows, (lo - at) * width), jnp.float32))
        head_t = assemble_t(
            all_block_cols[lo:hi], all_values_t[:, lo * width:hi * width], last, first
        )
        pieces.append(mdot(coupled_scaled[:, first * width:last * width], head_t, HIGH))
        at = hi
    if at < all_blocks:
        pieces.append(jnp.zeros((rows, (all_blocks - at) * width), jnp.float32))
    carried_next = next_block - jnp.concatenate(pieces, axis=1)

    fixed_panel = tdot(all_fixed[:, :factored], head_inverse, HIGH)
    own_fixed_panel = lax.dynamic_slice_in_dim(fixed_panel, top_at, rows, 1)
    fixed_factor = jnp.where(
        is_top, own_fixed_panel, fixed_rows - tdot(fixed_panel, lower, HIGH)
    )
    fixed_carried = fixed_next - tdot(fixed_panel, coupled_panel, HIGH)
    tip_next = tip_block - tdot(fixed_panel, fixed_panel, HIGH)
    return (factor_state, coupling_factor, carried_next, fixed_factor, fixed_carried, tip_next)


def solution(mesh):
    return jax.shard_map(
        on_device,
        mesh=mesh,
        in_specs=(
            P(("hyper", "row"), None),
            P(("hyper", "row"), None),
            P("row", None),
            P(("hyper", "row"), None),
            P("hyper", "row"),
            P("hyper", "row"),
            P("hyper", None),
        ),
        out_specs=(
            P(("hyper", "row"), None),
            P(("hyper", "row"), None),
            P(("hyper", "row"), None),
            P("hyper", "row"),
            P("hyper", "row"),
            P("hyper", None),
        ),
        check_vma=False,
    )
```

```python
import jax
import jax.numpy as jnp
from jax import lax
from jax.sharding import PartitionSpec as P

PANELS = 4
BLOCK = 128
REACH = 32
HIGHEST = lax.Precision.HIGHEST
HIGH = lax.Precision.HIGH


def mdot(left, right, precision=HIGHEST):
    return jnp.dot(left, right, precision=precision, preferred_element_type=jnp.float32)


def tdot(left, right, precision=HIGHEST):
    return lax.dot_general(
        left, right, (((1,), (1,)), ((), ())), precision=precision, preferred_element_type=jnp.float32
    )


def assemble_t(block_cols, values_t, col_blocks, first_block=0):
    block_rows, nonzero = block_cols.shape
    width = values_t.shape[0] // nonzero
    span = block_rows * width
    flipped = values_t.reshape(nonzero, 1, width, span)
    spread = jnp.repeat(block_cols.T, width, axis=1)
    columns = jnp.arange(first_block, col_blocks, dtype=jnp.int32)
    hit = spread[:, None, None, :] == columns[None, :, None, None]
    dense = jnp.where(hit, flipped, 0.0).sum(axis=0)
    return dense.reshape((col_blocks - first_block) * width, span)


def invert_lower(factor, block_inverses):
    inverses = jnp.stack(block_inverses)
    size = inverses.shape[1]
    while inverses.shape[0] > 1:
        pairs = inverses.shape[0] // 2
        first, second = inverses[0::2], inverses[1::2]
        coupling = jnp.stack(
            [
                factor[(2 * q + 1) * size:(2 * q + 2) * size, 2 * q * size:(2 * q + 1) * size]
                for q in range(pairs)
            ]
        )
        corner = jnp.einsum("qij,qjk->qik", second, coupling, precision=HIGHEST)
        corner = -jnp.einsum("qik,qkl->qil", corner, first, precision=HIGHEST)
        top = jnp.concatenate([first, jnp.zeros_like(first)], axis=2)
        bottom = jnp.concatenate([corner, second], axis=2)
        inverses = jnp.concatenate([top, bottom], axis=1)
        size *= 2
    return inverses[0]


def on_device(
    carried_block, coupling_values, block_cols, next_block, fixed_rows, fixed_next, tip_block
):
    rows, size = carried_block.shape
    value_rows, value_cols = coupling_values.shape
    local_block_rows, nonzero = block_cols.shape
    width = value_cols // nonzero
    fixed_count = fixed_rows.shape[0]
    factored = PANELS * rows
    me = lax.axis_index("row")
    is_top = me < PANELS
    top_at = jnp.minimum(me, PANELS - 1) * rows
    fixed_cols = fixed_rows.shape[1]
    block = min(BLOCK, rows)
    cols_count = local_block_rows * nonzero
    lanes = max(value_cols, fixed_cols, cols_count)

    def widen(part):
        return jnp.pad(part, ((0, 0), (0, lanes - part.shape[1])))

    values_t = coupling_values.T
    cols_row = block_cols.reshape(1, cols_count).astype(jnp.float32)
    packed = jnp.concatenate([widen(fixed_rows), widen(cols_row)], axis=0)
    pad = (-packed.shape[0]) % 8
    packed = jnp.concatenate([packed, jnp.zeros((pad, lanes), jnp.float32)], axis=0)
    gathered = lax.all_gather(packed, "row", axis=0)
    devices = gathered.shape[0]
    all_fixed = gathered[:, :fixed_count, :fixed_cols].transpose(1, 0, 2)
    all_fixed = all_fixed.reshape(fixed_count, devices * fixed_cols)
    all_block_cols = gathered[:, fixed_count, :cols_count]
    all_block_cols = jnp.round(all_block_cols).astype(jnp.int32).reshape(-1, nonzero)

    blocks = factored // block
    widths = [rows // block] * PANELS
    bounds = [0]
    for count in widths:
        bounds.append(bounds[-1] + count * block)
    chunks = [
        lax.all_gather(carried_block[:, lo:hi], "row", axis=0, tiled=True)
        for lo, hi in zip(bounds[:-1], bounds[1:])
    ]
    chunk_of = [c for c, count in enumerate(widths) for _ in range(count)]

    columns = []
    block_inverses = []
    for k in range(factored // block):
        chunk = chunk_of[k]
        offset = k * block - bounds[chunk]
        panel = chunks[chunk][k * block:factored, offset:offset + block]
        if k:
            done = jnp.concatenate([col[k * block:] for col in columns], axis=1)
            panel = panel - tdot(done, done[:block])
        diagonal = jnp.linalg.cholesky(panel[:block], symmetrize_input=False)
        diagonal_inverse = jax.scipy.linalg.solve_triangular(
            diagonal, jnp.eye(block, dtype=jnp.float32), lower=True
        )
        under = tdot(panel[block:], diagonal_inverse)
        column = jnp.concatenate(
            [jnp.zeros((k * block, block), jnp.float32), diagonal, under], axis=0
        )
        columns.append(column)
        block_inverses.append(diagonal_inverse)
    head_factor = jnp.concatenate(columns, axis=1)
    head_inverse = invert_lower(head_factor, block_inverses)

    def minus_below(scaled):
        total = None
        for c, (lo, hi) in enumerate(zip(bounds[:-1], bounds[1:])):
            part = tdot(scaled[:, lo:hi], chunks[c][factored:], HIGH)
            total = part if total is None else total + part
        return total

    own_cols = carried_block[:, :factored]
    lower = tdot(own_cols, head_inverse, HIGH)
    lower = jnp.where(is_top, lax.dynamic_slice_in_dim(head_factor, top_at, rows, 0), lower)
    lower_scaled = mdot(lower, head_inverse, HIGH)
    state_updates = jnp.pad(minus_below(lower_scaled), ((0, 0), (factored, 0)))
    factor_state = jnp.where(is_top, 0.0, carried_block - state_updates)
    factor_state = lax.dynamic_update_slice(factor_state, lower, (0, 0))

    coupled = assemble_t(block_cols, values_t, size // width).T
    coupled_panel = tdot(coupled[:, :factored], head_inverse, HIGH)
    coupled_scaled = mdot(coupled_panel, head_inverse, HIGH)
    coupled_updates = jnp.pad(minus_below(coupled_scaled), ((0, 0), (factored, 0)))
    coupling_factor = lax.dynamic_update_slice(coupled - coupled_updates, coupled_panel, (0, 0))

    all_values_t = lax.all_gather(values_t, "row", axis=1, tiled=True)
    all_blocks = size // width
    head_blocks = factored // width

    def reach(r):
        near = [n for n in range(head_blocks)
                if min(abs(n - r), all_blocks - abs(n - r)) <= REACH]
        return (min(near), max(near) + 1) if near else None

    groups = []
    for lo in range(0, all_blocks, 16):
        hi = min(lo + 16, all_blocks)
        hits = [reach(r) for r in range(lo, hi)]
        hits = [h for h in hits if h is not None]
        if not hits:
            continue
        cols = (min(h[0] for h in hits), max(h[1] for h in hits))
        if groups and groups[-1][1] == lo and groups[-1][2] == cols:
            groups[-1] = (groups[-1][0], hi, cols)
        else:
            groups.append((lo, hi, cols))
    pieces = []
    at = 0
    for lo, hi, (first, last) in groups:
        if lo > at:
            pieces.append(jnp.zeros((rows, (lo - at) * width), jnp.float32))
        skip = int(all(r < first or r >= last for r in range(lo, hi)))
        head_t = assemble_t(
            all_block_cols[lo:hi, skip:],
            all_values_t[skip * width:, lo * width:hi * width],
            last,
            first,
        )
        pieces.append(mdot(coupled_scaled[:, first * width:last * width], head_t, HIGH))
        at = hi
    if at < all_blocks:
        pieces.append(jnp.zeros((rows, (all_blocks - at) * width), jnp.float32))
    carried_next = next_block - jnp.concatenate(pieces, axis=1)

    fixed_panel = tdot(all_fixed[:, :factored], head_inverse, HIGH)
    own_fixed_panel = lax.dynamic_slice_in_dim(fixed_panel, top_at, rows, 1)
    fixed_factor = jnp.where(
        is_top, own_fixed_panel, fixed_rows - tdot(fixed_panel, lower, HIGH)
    )
    fixed_carried = fixed_next - tdot(fixed_panel, coupled_panel, HIGH)
    tip_next = tip_block - tdot(fixed_panel, fixed_panel, HIGH)
    return (factor_state, coupling_factor, carried_next, fixed_factor, fixed_carried, tip_next)


def solution(mesh):
    return jax.shard_map(
        on_device,
        mesh=mesh,
        in_specs=(
            P(("hyper", "row"), None),
            P(("hyper", "row"), None),
            P("row", None),
            P(("hyper", "row"), None),
            P("hyper", "row"),
            P("hyper", "row"),
            P("hyper", None),
        ),
        out_specs=(
            P(("hyper", "row"), None),
            P(("hyper", "row"), None),
            P(("hyper", "row"), None),
            P("hyper", "row"),
            P("hyper", "row"),
            P("hyper", None),
        ),
        check_vma=False,
    )
```

```python
import jax
import jax.numpy as jnp
from jax import lax
from jax.sharding import PartitionSpec as P

PANELS = 4
BLOCK = 128
REACH = 32
HIGHEST = lax.Precision.HIGHEST
HIGH = lax.Precision.HIGH


def mdot(left, right, precision=HIGHEST):
    return jnp.dot(left, right, precision=precision, preferred_element_type=jnp.float32)


def tdot(left, right, precision=HIGHEST):
    return lax.dot_general(
        left, right, (((1,), (1,)), ((), ())), precision=precision, preferred_element_type=jnp.float32
    )


def assemble_t(block_cols, values_t, col_blocks, first_block=0):
    block_rows, nonzero = block_cols.shape
    width = values_t.shape[0] // nonzero
    span = block_rows * width
    flipped = values_t.reshape(nonzero, 1, width, span)
    spread = jnp.repeat(block_cols.T, width, axis=1)
    columns = jnp.arange(first_block, col_blocks, dtype=jnp.int32)
    hit = spread[:, None, None, :] == columns[None, :, None, None]
    dense = jnp.where(hit, flipped, 0.0).sum(axis=0)
    return dense.reshape((col_blocks - first_block) * width, span)


def invert_lower(factor, block_inverses):
    inverses = jnp.stack(block_inverses)
    size = inverses.shape[1]
    while inverses.shape[0] > 1:
        pairs = inverses.shape[0] // 2
        first, second = inverses[0::2], inverses[1::2]
        coupling = jnp.stack(
            [
                factor[(2 * q + 1) * size:(2 * q + 2) * size, 2 * q * size:(2 * q + 1) * size]
                for q in range(pairs)
            ]
        )
        corner = jnp.einsum("qij,qjk->qik", second, coupling, precision=HIGHEST)
        corner = -jnp.einsum("qik,qkl->qil", corner, first, precision=HIGHEST)
        top = jnp.concatenate([first, jnp.zeros_like(first)], axis=2)
        bottom = jnp.concatenate([corner, second], axis=2)
        inverses = jnp.concatenate([top, bottom], axis=1)
        size *= 2
    return inverses[0]


def on_device(
    carried_block, coupling_values, block_cols, next_block, fixed_rows, fixed_next, tip_block
):
    rows, size = carried_block.shape
    value_rows, value_cols = coupling_values.shape
    local_block_rows, nonzero = block_cols.shape
    width = value_cols // nonzero
    fixed_count = fixed_rows.shape[0]
    factored = PANELS * rows
    me = lax.axis_index("row")
    is_top = me < PANELS
    top_at = jnp.minimum(me, PANELS - 1) * rows
    fixed_cols = fixed_rows.shape[1]
    block = min(BLOCK, rows)
    cols_count = local_block_rows * nonzero
    lanes = max(value_cols, fixed_cols, cols_count)

    def widen(part):
        return jnp.pad(part, ((0, 0), (0, lanes - part.shape[1])))

    values_t = coupling_values.T
    cols_row = block_cols.reshape(1, cols_count).astype(jnp.float32)
    packed = jnp.concatenate([widen(fixed_rows), widen(cols_row)], axis=0)
    pad = (-packed.shape[0]) % 8
    packed = jnp.concatenate([packed, jnp.zeros((pad, lanes), jnp.float32)], axis=0)
    gathered = lax.all_gather(packed, "row", axis=0)
    devices = gathered.shape[0]
    all_fixed = gathered[:, :fixed_count, :fixed_cols].transpose(1, 0, 2)
    all_fixed = all_fixed.reshape(fixed_count, devices * fixed_cols)
    all_block_cols = gathered[:, fixed_count, :cols_count]
    all_block_cols = jnp.round(all_block_cols).astype(jnp.int32).reshape(-1, nonzero)

    blocks = factored // block
    widths = [rows // block] * PANELS
    bounds = [0]
    for count in widths:
        bounds.append(bounds[-1] + count * block)
    chunks = [
        lax.all_gather(carried_block[:, lo:hi], "row", axis=0, tiled=True)
        for lo, hi in zip(bounds[:-1], bounds[1:])
    ]
    chunk_of = [c for c, count in enumerate(widths) for _ in range(count)]

    columns = []
    block_inverses = []
    for k in range(factored // block):
        chunk = chunk_of[k]
        offset = k * block - bounds[chunk]
        panel = chunks[chunk][k * block:factored, offset:offset + block]
        if k:
            done = jnp.concatenate([col[k * block:] for col in columns], axis=1)
            panel = panel - tdot(done, done[:block])
        diagonal = jnp.linalg.cholesky(panel[:block], symmetrize_input=False)
        diagonal_inverse = jax.scipy.linalg.solve_triangular(
            diagonal, jnp.eye(block, dtype=jnp.float32), lower=True
        )
        under = tdot(panel[block:], diagonal_inverse)
        column = jnp.concatenate(
            [jnp.zeros((k * block, block), jnp.float32), diagonal, under], axis=0
        )
        columns.append(column)
        block_inverses.append(diagonal_inverse)
    head_factor = jnp.concatenate(columns, axis=1)
    head_inverse = invert_lower(head_factor, block_inverses)

    def minus_below(scaled):
        total = None
        for c, (lo, hi) in enumerate(zip(bounds[:-1], bounds[1:])):
            part = tdot(scaled[:, lo:hi], chunks[c][factored:], HIGH)
            total = part if total is None else total + part
        return total

    own_cols = carried_block[:, :factored]
    lower = tdot(own_cols, head_inverse, HIGH)
    lower = jnp.where(is_top, lax.dynamic_slice_in_dim(head_factor, top_at, rows, 0), lower)
    lower_scaled = mdot(lower, head_inverse, HIGH)
    state_updates = jnp.pad(minus_below(lower_scaled), ((0, 0), (factored, 0)))
    factor_state = jnp.where(is_top, 0.0, carried_block - state_updates)
    factor_state = lax.dynamic_update_slice(factor_state, lower, (0, 0))

    coupled = assemble_t(block_cols, values_t, size // width).T
    coupled_panel = tdot(coupled[:, :factored], head_inverse, HIGH)
    coupled_scaled = mdot(coupled_panel, head_inverse, HIGH)
    coupled_updates = jnp.pad(minus_below(coupled_scaled), ((0, 0), (factored, 0)))
    coupling_factor = lax.dynamic_update_slice(coupled - coupled_updates, coupled_panel, (0, 0))

    all_values_t = lax.all_gather(values_t, "row", axis=1, tiled=True)
    all_blocks = size // width
    head_blocks = factored // width

    def reach(r):
        near = [n for n in range(head_blocks)
                if min(abs(n - r), all_blocks - abs(n - r)) <= REACH]
        return (min(near), max(near) + 1) if near else None

    groups = []
    for lo in range(0, all_blocks, 16):
        hi = min(lo + 16, all_blocks)
        hits = [reach(r) for r in range(lo, hi)]
        hits = [h for h in hits if h is not None]
        if not hits:
            continue
        cols = (min(h[0] for h in hits), max(h[1] for h in hits))
        cols = cols + (int(all(r < cols[0] or r >= cols[1] for r in range(lo, hi))),)
        if groups and groups[-1][1] == lo and groups[-1][2] == cols:
            groups[-1] = (groups[-1][0], hi, cols)
        else:
            groups.append((lo, hi, cols))
    pieces = []
    at = 0
    for lo, hi, (first, last, skip) in groups:
        if lo > at:
            pieces.append(jnp.zeros((rows, (lo - at) * width), jnp.float32))
        head_t = assemble_t(
            all_block_cols[lo:hi, skip:],
            all_values_t[skip * width:, lo * width:hi * width],
            last,
            first,
        )
        pieces.append(mdot(coupled_scaled[:, first * width:last * width], head_t, HIGH))
        at = hi
    if at < all_blocks:
        pieces.append(jnp.zeros((rows, (all_blocks - at) * width), jnp.float32))
    carried_next = next_block - jnp.concatenate(pieces, axis=1)

    fixed_panel = tdot(all_fixed[:, :factored], head_inverse, HIGH)
    own_fixed_panel = lax.dynamic_slice_in_dim(fixed_panel, top_at, rows, 1)
    fixed_factor = jnp.where(
        is_top, own_fixed_panel, fixed_rows - tdot(fixed_panel, lower, HIGH)
    )
    fixed_carried = fixed_next - tdot(fixed_panel, coupled_panel, HIGH)
    tip_next = tip_block - tdot(fixed_panel, fixed_panel, HIGH)
    return (factor_state, coupling_factor, carried_next, fixed_factor, fixed_carried, tip_next)


def solution(mesh):
    return jax.shard_map(
        on_device,
        mesh=mesh,
        in_specs=(
            P(("hyper", "row"), None),
            P(("hyper", "row"), None),
            P("row", None),
            P(("hyper", "row"), None),
            P("hyper", "row"),
            P("hyper", "row"),
            P("hyper", None),
        ),
        out_specs=(
            P(("hyper", "row"), None),
            P(("hyper", "row"), None),
            P(("hyper", "row"), None),
            P("hyper", "row"),
            P("hyper", "row"),
            P("hyper", None),
        ),
        check_vma=False,
    )
```
